256 devices in a mesh: tm: 128 (over z, x_lo, y, core), head: 2 (over x_hi).
Axes of the slice: x: 4 (x_hi: 2, x_lo: 2; x = x_hi * 2 + x_lo), y: 4, z: 8, core: 2. Of those that a mesh axis runs over, the one named last changes fastest.
Arguments:
- queries: bfloat16 [32768, 2048], P('tm', 'head'), may hold values from -48 to 48
- keys: bfloat16 [32768, 2048], P('tm', 'head'), may hold values from -6 to 6
- values_in: bfloat16 [32768, 2048], P('tm', 'head'), may hold values from -32 to 32
- teacher: bfloat16 [32768, 2048], P('tm', 'head'), may hold values from -6 to 6
- gain: float32 [2048], P('head'), may hold values from 0.25 to 1.75
- conv_weight: float32 [4, 2048], P(None, 'head'), may hold values from -3 to 3
- block_bits: int32 [256, 6], P('tm'), may hold values from 0 to 1, as said below
- mask_pos: int32 [256, 64], P('tm'), may hold values from 0 to 127, as said below
Outputs:
- query_grad: bfloat16 [32768, 2048], P('tm', 'head')
- key_grad: bfloat16 [32768, 2048], P('tm', 'head')
- value_grad: bfloat16 [32768, 2048], P('tm', 'head')
- conv_grad: float32 [4, 2048], P(None, 'head')
The draws below stay inside these ranges and needn't reach their ends.
Inputs may be any that keep to these rules, and one draw needn't show every extreme that they name: `block_bits`: column 0 of every row is 1. `mask_pos`: each row names 64 different positions.
All inputs are finite; a program needn't handle non-finite values.
Results may differ from the reference program's by a relative error of at most 0.0095.
Values may be sent and summed in bfloat16 or wider, within the bound.
No kernel may reach another device: no remote copies, remote signals or barrier semaphores. Data moves between devices by JAX's collectives and lax.ppermute only.
A program may use at most 64 MiB of HBM per device.

```python
import jax
import jax.numpy as jnp
from jax import lax

D = 2048
HEADS = 16
HD = 128
TOK_DEV = 256
BLK = 128
KW = 4
MPB = 64
REACH = 3
TOKENS = 32768
NBLK = 256
WIN = 6
N_TM = 128


def query_key_pair(key):
    base_query = jax.random.fold_in(key, 101)
    base_key = jax.random.fold_in(key, 202)
    query_all = jnp.clip(jax.random.normal(base_query, (TOKENS, D), jnp.float32), -6.0, 6.0)
    key_all = jnp.clip(jax.random.normal(base_key, (TOKENS, D), jnp.float32), -6.0, 6.0)
    return (query_all, key_all)


def draw_queries(key, part):
    return query_key_pair(key)[0].astype(jnp.bfloat16)


def draw_keys(key, part):
    return query_key_pair(key)[1].astype(jnp.bfloat16)


def draw_values_in(key, part):
    channel = jnp.arange(D, dtype=jnp.float32)
    channel_scale = 0.6 * 3.0 ** (channel / (D - 1))
    drawn = jnp.clip(jax.random.normal(jax.random.fold_in(key, 7), (TOKENS, D), jnp.float32), -6.0, 6.0) * channel_scale[None, :]
    return drawn.astype(jnp.bfloat16)


def draw_block_bits(key, part):
    device_count = TOKENS // TOK_DEV
    density_level = jax.random.randint(jax.random.fold_in(key, 1), (device_count,), 0, 8)
    row_level = jnp.repeat(density_level, TOK_DEV // BLK)
    random_draws = jax.random.randint(jax.random.fold_in(key, 2), (NBLK, WIN), 0, 8)
    block_flags = (random_draws <= row_level[:, None]).astype(jnp.int32)
    column = jnp.arange(WIN, dtype=jnp.int32)
    return jnp.where(column[None, :] == 0, 1, block_flags).astype(jnp.int32)


def draw_mask_pos(key, part):
    key_list = jax.random.split(key, NBLK)

    def one_block(sub_key):
        return jax.random.permutation(sub_key, BLK)[:MPB]
    return jax.vmap(one_block)(key_list).astype(jnp.int32)


def shard_levels(key, shape, cuts, least, largest):
    def one(dim, shards_of):
        steps = jax.random.uniform(jax.random.fold_in(jax.random.fold_in(key, 6), dim), (shards_of,), jnp.float32, least / len(cuts), largest / len(cuts))
        return jnp.repeat(jnp.exp(steps), shape[dim] // shards_of).reshape((-1,) + (1,) * (len(shape) - dim - 1))

    factor_of = one(*cuts[0])
    for cut in cuts[1:]:
        factor_of = factor_of * one(*cut)
    return factor_of


def noise(own_key, dims, spread, reach, cuts=(), kind=jnp.bfloat16):
    values = spread * jax.random.normal(own_key, dims, jnp.float32)
    if cuts:
        values = values * shard_levels(own_key, dims, cuts, -0.22, 0.18)
    return jnp.clip(values, -reach, reach).astype(kind)


def setup_inputs(seed: int = 0) -> dict:
    arg_keys = jax.random.split(jax.random.key(seed), 9)
    queries = draw_queries(jax.random.fold_in(arg_keys[8], 71), 0)
    keys = draw_keys(jax.random.fold_in(arg_keys[8], 71), 0)
    values_in = draw_values_in(jax.random.fold_in(arg_keys[8], 71), 0)
    teacher = noise(arg_keys[3], (TOKENS, D), 1.0, 6.0, ((0, 128), (1, 2)))
    gain = jnp.clip(1.0 + 0.15 * jax.random.normal(arg_keys[4], (D,), jnp.float32), 0.25, 1.75)
    conv_weight = noise(arg_keys[5], (KW, D), 0.5, 3.0, ((1, 2),), jnp.float32)
    block_bits = draw_block_bits(jax.random.fold_in(arg_keys[8], 71), 0)
    mask_pos = draw_mask_pos(jax.random.fold_in(arg_keys[8], 71), 0)
    return dict(queries=queries, keys=keys, values_in=values_in, teacher=teacher, gain=gain, conv_weight=conv_weight, block_bits=block_bits, mask_pos=mask_pos)


NEG_FILL = -1e+30
NORM_EPS = 1e-06

def split_heads(array):
    return array.reshape(array.shape[0], HEADS, HD)

def device_rows(array, device):
    return lax.dynamic_slice_in_dim(array, jnp.clip(device, 0, N_TM - 1) * TOK_DEV, TOK_DEV, 0)

def pair_mask(block_bits, qdevice, kdevice):
    qpos = qdevice * TOK_DEV + jnp.arange(TOK_DEV, dtype=jnp.int32)
    kpos = kdevice * TOK_DEV + jnp.arange(TOK_DEV, dtype=jnp.int32)
    relative = qpos[:, None] // BLK - kpos[None, :] // BLK
    bit_rows = lax.dynamic_slice_in_dim(block_bits, jnp.clip(qdevice, 0, N_TM - 1) * (TOK_DEV // BLK), TOK_DEV // BLK, 0)
    bit_rows = jnp.repeat(bit_rows, BLK, axis=0)
    picked = jnp.take_along_axis(bit_rows, jnp.clip(relative, 0, WIN - 1).astype(jnp.int32), axis=1)
    return (kdevice >= 0) & (qdevice < N_TM) & (kpos[None, :] <= qpos[:, None]) & (relative < WIN) & (picked > 0)

def reference(queries, keys, values_in, teacher, gain, conv_weight, block_bits, mask_pos):
    score_scale = HD ** (-0.5)
    padded_in = jnp.concatenate([jnp.zeros((KW - 1, D), jnp.float32), values_in.astype(jnp.float32)], 0)
    conv_sum = jnp.zeros((TOKENS, D), jnp.float32)
    for tap_index in range(KW):
        conv_sum = conv_sum + conv_weight[tap_index] * padded_in[KW - 1 - tap_index:KW - 1 - tap_index + TOKENS]
    values = conv_sum.astype(jnp.bfloat16)
    query_f = queries.astype(jnp.float32)
    key_f = keys.astype(jnp.float32)
    value_f = values.astype(jnp.float32)

    def pair_scores(qdevice, kdevice):
        raw_scores = jnp.einsum('thd,uhd->htu', split_heads(device_rows(query_f, qdevice)), split_heads(device_rows(key_f, kdevice))) * score_scale
        allowed = pair_mask(block_bits, qdevice, kdevice)
        return (jnp.where(allowed[None], raw_scores, NEG_FILL), allowed)

    def forward_block(qdevice):
        pairs = [pair_scores(qdevice, qdevice - distance) for distance in range(REACH + 1)]
        row_peak = lax.optimization_barrier(jnp.max(pairs[0][0], axis=2))
        for distance in range(1, REACH + 1):
            row_peak = jnp.maximum(row_peak, lax.optimization_barrier(jnp.max(pairs[distance][0], axis=2)))
        expos = [jnp.where(allowed[None], jnp.exp(scores - row_peak[..., None]), 0.0) for scores, allowed in pairs]
        row_total = jnp.zeros_like(row_peak)
        for distance in range(REACH + 1):
            row_total = row_total + lax.optimization_barrier(jnp.sum(expos[distance], axis=2))
        attended = jnp.zeros((TOK_DEV, HEADS, HD), jnp.float32)
        for distance in range(REACH + 1):
            weights = (expos[distance] / row_total[..., None]).astype(jnp.bfloat16).astype(jnp.float32)
            attended = attended + jnp.einsum('htu,uhd->thd', weights, split_heads(device_rows(value_f, qdevice - distance)))
        return (attended.reshape(TOK_DEV, D), row_peak, row_total)
    attended, peaks, totals = lax.map(forward_block, jnp.arange(N_TM, dtype=jnp.int32))
    attended = attended.reshape(TOKENS, D)
    squares = lax.optimization_barrier(jnp.sum(attended * attended, axis=1))
    inverse = lax.rsqrt(squares / D + NORM_EPS)
    prediction = attended * inverse[:, None] * gain
    position = jnp.arange(TOKENS, dtype=jnp.int32) % BLK
    chosen = jnp.any(jnp.repeat(mask_pos, BLK, axis=0) == position[:, None], axis=1)
    residual = jnp.where(chosen[:, None], prediction - teacher.astype(jnp.float32), 0.0)
    scaled = residual * gain
    cross_term = lax.optimization_barrier(jnp.sum(scaled * attended, axis=1))
    out_grad = (inverse[:, None] * scaled - attended * (inverse ** 3 * cross_term / D)[:, None]).astype(jnp.bfloat16)
    grad_f = out_grad.astype(jnp.float32)
    delta = lax.optimization_barrier(jnp.sum((grad_f * attended).reshape(TOKENS, HEADS, HD), axis=2))

    def pair_prob(qdevice, kdevice):
        scores, allowed = pair_scores(qdevice, kdevice)
        clipped = jnp.clip(qdevice, 0, N_TM - 1)
        expo = jnp.where(allowed[None], jnp.exp(scores - peaks[clipped][..., None]), 0.0)
        return expo / totals[clipped][..., None]

    def score_grad_of(qdevice, kdevice):
        prob = pair_prob(qdevice, kdevice)
        prob_grad = jnp.einsum('thd,uhd->htu', split_heads(device_rows(grad_f, qdevice)), split_heads(device_rows(value_f, kdevice)))
        score_grad = (prob * (prob_grad - device_rows(delta, qdevice).T[..., None])).astype(jnp.bfloat16).astype(jnp.float32)
        return (prob, score_grad)

    def query_block(qdevice):
        grad_block = jnp.zeros((TOK_DEV, HEADS, HD), jnp.float32)
        for distance in range(REACH + 1):
            kdevice = qdevice - distance
            prob, score_grad = score_grad_of(qdevice, kdevice)
            grad_block = grad_block + jnp.einsum('htu,uhd->thd', score_grad, split_heads(device_rows(key_f, kdevice))) * score_scale
        return grad_block.reshape(TOK_DEV, D)

    def key_block(kdevice):
        grad_keys = jnp.zeros((TOK_DEV, HEADS, HD), jnp.float32)
        grad_values = jnp.zeros((TOK_DEV, HEADS, HD), jnp.float32)
        for distance in range(REACH + 1):
            qdevice = kdevice + distance
            prob, score_grad = score_grad_of(qdevice, kdevice)
            grad_keys = grad_keys + jnp.einsum('htu,thd->uhd', score_grad, split_heads(device_rows(query_f, qdevice))) * score_scale
            weights = prob.astype(jnp.bfloat16).astype(jnp.float32)
            grad_values = grad_values + jnp.einsum('htu,thd->uhd', weights, split_heads(device_rows(grad_f, qdevice)))
        return (grad_keys.reshape(TOK_DEV, D), grad_values.reshape(TOK_DEV, D))
    query_grad = lax.map(query_block, jnp.arange(N_TM, dtype=jnp.int32)).reshape(TOKENS, D).astype(jnp.bfloat16)
    key_parts, value_parts = lax.map(key_block, jnp.arange(N_TM, dtype=jnp.int32))
    key_grad = key_parts.reshape(TOKENS, D).astype(jnp.bfloat16)
    value_acc = value_parts.reshape(TOKENS, D)
    padded_acc = jnp.concatenate([value_acc, jnp.zeros((KW - 1, D), jnp.float32)], 0)
    value_sum = jnp.zeros((TOKENS, D), jnp.float32)
    for tap_index in range(KW):
        value_sum = value_sum + conv_weight[tap_index] * padded_acc[tap_index:tap_index + TOKENS]
    value_grad = value_sum.astype(jnp.bfloat16)
    conv_grad = jnp.stack([lax.optimization_barrier(jnp.sum(value_acc * padded_in[KW - 1 - tap_index:KW - 1 - tap_index + TOKENS], axis=0)) for tap_index in range(KW)])
    return (query_grad, key_grad, value_grad, conv_grad)
```

```python
from functools import reduce

import jax
import jax.numpy as jnp
from jax import lax
from jax.sharding import PartitionSpec as P

D = 2048
HD = 128
BLK = 128
REACH = 3


NEG_FILL = -1e30
NORM_EPS = 1e-06


def from_behind(block, axis, distance):
    devices = range(lax.axis_size(axis))
    route = [(i - distance, i) for i in devices if i - distance in devices]
    return lax.ppermute(block, axis, route)


def all_sum(block, axis):
    size = lax.axis_size(axis)
    if size & (size - 1):
        return lax.psum(block, axis)
    stride = 1
    while stride < size:
        block = block + lax.ppermute(block, axis, [(i, i ^ stride) for i in range(size)])
        stride *= 2
    return block


def split_heads(array):
    return array.reshape(array.shape[0], array.shape[1] // HD, HD)


def pair_mask(block_bits, device, distance, row_count):
    per_device = row_count // BLK
    window = block_bits.shape[1]
    block_index = jnp.arange(per_device, dtype=jnp.int32)
    relative = distance * per_device + block_index[:, None] - block_index[None, :]
    one_hot = relative[:, :, None] == jnp.arange(window, dtype=jnp.int32)[None, None, :]
    picked_bits = jnp.sum(jnp.where(one_hot, block_bits[:, None, :], 0), axis=2)
    coarse_mask = (picked_bits > 0) & (relative < window)
    fine_mask = jnp.repeat(jnp.repeat(coarse_mask, BLK, axis=0), BLK, axis=1)
    offsets = jnp.arange(row_count, dtype=jnp.int32)
    causal = (distance > 0) | (offsets[None, :] <= offsets[:, None])
    return fine_mask & causal & (device >= distance)


def body(queries, keys, values_in, teacher, gain, conv_weight, block_bits, mask_pos):
    row_count, channels = queries.shape
    tap_count = conv_weight.shape[0]
    rim_rows = tap_count - 1
    device = lax.axis_index("tm")
    score_scale = HD ** (-0.5)
    prior = from_behind(values_in[row_count - rim_rows :], "tm", 1)
    extended = jnp.concatenate([prior, values_in], 0).astype(jnp.float32)
    conv_sum = jnp.zeros((row_count, channels), jnp.float32)
    for tap_index in range(tap_count):
        conv_sum = (
            conv_sum
            + conv_weight[tap_index]
            * extended[rim_rows - tap_index : rim_rows - tap_index + row_count]
        )
    values = conv_sum.astype(jnp.bfloat16)
    blocks = [(keys, values)]
    for distance in range(1, REACH + 1):
        moved_keys, moved_values = from_behind((keys, values), "tm", distance)
        blocks.append((moved_keys, moved_values))
    heads_query = split_heads(queries)
    pair_masks = [
        pair_mask(block_bits, device, distance, row_count) for distance in range(REACH + 1)
    ]
    scores = []
    for distance in range(REACH + 1):
        raw_scores = (
            jnp.einsum(
                "thd,uhd->htu",
                heads_query,
                split_heads(blocks[distance][0]),
                preferred_element_type=jnp.float32,
            )
            * score_scale
        )
        scores.append(jnp.where(pair_masks[distance][None], raw_scores, NEG_FILL))
    row_peak = reduce(jnp.maximum, [jnp.max(block_scores, axis=2) for block_scores in scores])
    expos = [
        jnp.where(pair_masks[distance][None], jnp.exp(scores[distance] - row_peak[..., None]), 0.0)
        for distance in range(REACH + 1)
    ]
    row_total = reduce(jnp.add, [jnp.sum(expo_block, axis=2) for expo_block in expos])
    probs = [expo_block / row_total[..., None] for expo_block in expos]
    attended = jnp.zeros((row_count, channels // HD, HD), jnp.float32)
    for distance in range(REACH + 1):
        weights = probs[distance].astype(jnp.bfloat16)
        attended = attended + jnp.einsum(
            "htu,uhd->thd",
            weights,
            split_heads(blocks[distance][1]),
            preferred_element_type=jnp.float32,
        )
    flattened = attended.reshape(row_count, channels)
    squares = lax.psum(jnp.sum(flattened * flattened, axis=1), "head")
    inverse = lax.rsqrt(squares / D + NORM_EPS)
    prediction = flattened * inverse[:, None] * gain
    position = jnp.arange(row_count, dtype=jnp.int32) % BLK
    chosen = jnp.any(jnp.repeat(mask_pos, BLK, axis=0) == position[:, None], axis=1)
    residual = jnp.where(chosen[:, None], prediction - teacher.astype(jnp.float32), 0.0)
    scaled = residual * gain
    cross_term = lax.psum(jnp.sum(scaled * flattened, axis=1), "head")
    out_grad = (
        inverse[:, None] * scaled - flattened * (inverse**3 * cross_term / D)[:, None]
    ).astype(jnp.bfloat16)
    heads_grad = split_heads(out_grad)
    delta = jnp.sum(heads_grad.astype(jnp.float32) * attended, axis=2).T
    query_acc = jnp.zeros((row_count, channels // HD, HD), jnp.float32)
    partials = []
    for distance in range(REACH + 1):
        block_keys, block_values = blocks[distance]
        prob = probs[distance]
        prob_grad = jnp.einsum(
            "thd,uhd->htu",
            heads_grad,
            split_heads(block_values),
            preferred_element_type=jnp.float32,
        )
        score_grad = (prob * (prob_grad - delta[:, :, None])).astype(jnp.bfloat16)
        query_acc = (
            query_acc
            + jnp.einsum(
                "htu,uhd->thd",
                score_grad,
                split_heads(block_keys),
                preferred_element_type=jnp.float32,
            )
            * score_scale
        )
        key_part = (
            jnp.einsum("htu,thd->uhd", score_grad, heads_query, preferred_element_type=jnp.float32)
            * score_scale
        )
        value_part = jnp.einsum(
            "htu,thd->uhd",
            prob.astype(jnp.bfloat16),
            heads_grad,
            preferred_element_type=jnp.float32,
        )
        partials.append(
            (key_part.reshape(row_count, channels), value_part.reshape(row_count, channels))
        )
    key_acc, value_acc = partials[0]
    for distance in range(1, REACH + 1):
        back_keys, back_values = (
            from_behind(partials[distance][0].astype(jnp.bfloat16), "tm", -distance).astype(
                jnp.float32
            ),
            from_behind(partials[distance][1].astype(jnp.bfloat16), "tm", -distance).astype(
                jnp.float32
            ),
        )
        key_acc = key_acc + back_keys
        value_acc = value_acc + back_values
    following = from_behind(value_acc[:rim_rows], "tm", -1)
    padded_acc = jnp.concatenate([value_acc, following], 0)
    value_sum = jnp.zeros((row_count, channels), jnp.float32)
    for tap_index in range(tap_count):
        value_sum = (
            value_sum + conv_weight[tap_index] * padded_acc[tap_index : tap_index + row_count]
        )
    local_taps = jnp.stack(
        [
            jnp.sum(
                value_acc * extended[rim_rows - tap_index : rim_rows - tap_index + row_count],
                axis=0,
            )
            for tap_index in range(tap_count)
        ]
    )
    conv_grad = all_sum(local_taps, "tm")
    return (
        query_acc.reshape(row_count, channels).astype(jnp.bfloat16),
        key_acc.astype(jnp.bfloat16),
        value_sum.astype(jnp.bfloat16),
        conv_grad,
    )


def solution(mesh):
    placed = (
        P("tm", "head"),
        P("tm", "head"),
        P("tm", "head"),
        P("tm", "head"),
        P("head"),
        P(None, "head"),
        P("tm", None),
        P("tm", None),
    )
    return jax.shard_map(
        body,
        mesh=mesh,
        in_specs=placed,
        out_specs=(P("tm", "head"), P("tm", "head"), P("tm", "head"), P(None, "head")),
        check_vma=False,
    )
```

```python
import jax
import jax.numpy as jnp
from jax import lax
from jax.sharding import PartitionSpec as P

D = 2048
HD = 128
BLK = 128
REACH = 3
WIN = 6


NEG_FILL = -1e30
NORM_EPS = 1e-06


def from_behind(block, axis, distance):
    devices = range(lax.axis_size(axis))
    route = [(i - distance, i) for i in devices if i - distance in devices]
    return lax.ppermute(block, axis, route)


def chip_swap(block, axis):
    size = lax.axis_size(axis)
    return lax.ppermute(block, axis, [(i, i ^ 1) for i in range(size)])


def all_sum(block, axis):
    size = lax.axis_size(axis)
    if size & (size - 1):
        return lax.psum(block, axis)
    stride = 1
    while stride < size:
        block = block + lax.ppermute(block, axis, [(i, i ^ stride) for i in range(size)])
        stride *= 2
    return block


def pair_sum(block, axis):
    if lax.axis_size(axis) != 2:
        return lax.psum(block, axis)
    return block + lax.ppermute(block, axis, [(0, 1), (1, 0)])


def split_heads(array):
    return array.reshape(array.shape[0], array.shape[1] // HD, HD)


def window_mask(block_bits, device, row_count, key_count):
    per_device = row_count // BLK
    key_blocks = key_count // BLK
    first_block = device * per_device - (key_blocks - per_device)
    qb = jnp.arange(per_device, dtype=jnp.int32)
    kb = jnp.arange(key_blocks, dtype=jnp.int32)
    relative = qb[:, None] + (key_blocks - per_device) - kb[None, :]
    one_hot = relative[:, :, None] == jnp.arange(WIN, dtype=jnp.int32)[None, None, :]
    picked_bits = jnp.sum(jnp.where(one_hot, block_bits[:, None, :], 0), axis=2)
    coarse = (picked_bits > 0) & (relative >= 0) & (relative < WIN) & (first_block + kb[None, :] >= 0)
    fine = jnp.repeat(jnp.repeat(coarse, BLK, axis=0), BLK, axis=1)
    q = jnp.arange(row_count, dtype=jnp.int32)
    s = jnp.arange(key_count, dtype=jnp.int32)
    causal = s[None, :] <= q[:, None] + (key_count - row_count)
    return fine & causal


def body(queries, keys, values_in, teacher, gain, conv_weight, block_bits, mask_pos):
    row_count, channels = queries.shape
    tap_count = conv_weight.shape[0]
    rim_rows = tap_count - 1
    device = lax.axis_index("tm")
    even = device % 2 == 0
    score_scale = HD ** (-0.5)
    far_rows = row_count - BLK
    far_lead = 8
    key_count = REACH * row_count + (row_count - far_rows)

    own = jnp.concatenate([keys, values_in], 1)
    second = from_behind(own, "tm", 2)
    first = chip_swap(jnp.where(even, own, second), "tm")
    third = from_behind(second[far_rows - far_lead :], "tm", 1)
    window = jnp.concatenate([third, second, first, own], 0)
    key_win = window[far_lead:, :channels]
    vin_win = window[:, channels:].astype(jnp.float32)

    conv_sum = jnp.zeros((key_count, channels), jnp.float32)
    for tap_index in range(tap_count):
        conv_sum = conv_sum + conv_weight[tap_index] * vin_win[far_lead - tap_index : far_lead - tap_index + key_count]
    value_win = conv_sum.astype(jnp.bfloat16)

    heads_query = split_heads(queries)
    heads_key = split_heads(key_win)
    heads_value = split_heads(value_win)
    mask = window_mask(block_bits, device, row_count, key_count)

    raw_scores = (
        jnp.einsum("thd,uhd->htu", heads_query, heads_key, preferred_element_type=jnp.float32)
        * score_scale
    )
    scores = jnp.where(mask[None], raw_scores, NEG_FILL)
    row_peak = jnp.max(scores, axis=2)
    expo = jnp.where(mask[None], jnp.exp(scores - row_peak[..., None]), 0.0)
    row_total = jnp.sum(expo, axis=2)
    prob = expo / row_total[..., None]
    weights = prob.astype(jnp.bfloat16)
    attended = jnp.einsum("htu,uhd->thd", weights, heads_value, preferred_element_type=jnp.float32)

    flattened = attended.reshape(row_count, channels)
    squares = pair_sum(jnp.sum(flattened * flattened, axis=1), "head")
    inverse = lax.rsqrt(squares / D + NORM_EPS)
    prediction = flattened * inverse[:, None] * gain
    position = jnp.arange(row_count, dtype=jnp.int32) % BLK
    chosen = jnp.any(jnp.repeat(mask_pos, BLK, axis=0) == position[:, None], axis=1)
    residual = jnp.where(chosen[:, None], prediction - teacher.astype(jnp.float32), 0.0)
    scaled = residual * gain
    cross_term = pair_sum(jnp.sum(scaled * flattened, axis=1), "head")
    out_grad = (
        inverse[:, None] * scaled - flattened * (inverse**3 * cross_term / D)[:, None]
    ).astype(jnp.bfloat16)
    heads_grad = split_heads(out_grad)
    delta = jnp.sum(heads_grad.astype(jnp.float32) * attended, axis=2).T

    prob_grad = jnp.einsum("thd,uhd->htu", heads_grad, heads_value, preferred_element_type=jnp.float32)
    score_grad = (prob * (prob_grad - delta[:, :, None])).astype(jnp.bfloat16)
    query_grad = (
        jnp.einsum("htu,uhd->thd", score_grad, heads_key, preferred_element_type=jnp.float32)
        * score_scale
    )
    key_part = (
        jnp.einsum("htu,thd->uhd", score_grad, heads_query, preferred_element_type=jnp.float32)
        * score_scale
    ).reshape(key_count, channels)
    value_part = jnp.einsum(
        "htu,thd->uhd", weights, heads_grad, preferred_element_type=jnp.float32
    ).reshape(key_count, channels)

    local_taps = jnp.stack(
        [
            jnp.sum(value_part * vin_win[far_lead - tap_index : far_lead - tap_index + key_count], axis=0)
            for tap_index in range(tap_count)
        ]
    )
    conv_grad = all_sum(local_taps, "tm")

    lead = jnp.zeros((far_lead, channels), jnp.float32)
    padded_value = jnp.concatenate([lead, value_part, jnp.zeros((rim_rows, channels), jnp.float32)], 0)
    value_sum = jnp.zeros((key_count + far_lead, channels), jnp.float32)
    for tap_index in range(tap_count):
        value_sum = value_sum + conv_weight[tap_index] * padded_value[tap_index : tap_index + key_count + far_lead]
    grads = jnp.concatenate([jnp.concatenate([lead, key_part], 0), value_sum], 1)

    cut_third = row_count - far_rows + far_lead
    grad_third = grads[:cut_third]
    grad_second = grads[cut_third : cut_third + row_count]
    grad_first = grads[cut_third + row_count : cut_third + 2 * row_count]
    grad_own = grads[cut_third + 2 * row_count :]

    back_third = from_behind(grad_third.astype(jnp.bfloat16), "tm", -1).astype(jnp.float32)
    back_first = chip_swap(grad_first.astype(jnp.bfloat16), "tm").astype(jnp.float32)
    grad_second = grad_second + jnp.concatenate(
        [jnp.zeros((far_rows - far_lead, 2 * channels), jnp.float32), back_third], 0
    )
    grad_second = grad_second + jnp.where(even, 0.0, back_first)
    back_second = from_behind(grad_second.astype(jnp.bfloat16), "tm", -2).astype(jnp.float32)
    total = grad_own + jnp.where(even, back_first, 0.0) + back_second

    return (
        query_grad.reshape(row_count, channels).astype(jnp.bfloat16),
        total[:, :channels].astype(jnp.bfloat16),
        total[:, channels:].astype(jnp.bfloat16),
        conv_grad,
    )


def solution(mesh):
    placed = (
        P("tm", "head"),
        P("tm", "head"),
        P("tm", "head"),
        P("tm", "head"),
        P("head"),
        P(None, "head"),
        P("tm", None),
        P("tm", None),
    )
    return jax.shard_map(
        body,
        mesh=mesh,
        in_specs=placed,
        out_specs=(P("tm", "head"), P("tm", "head"), P("tm", "head"), P(None, "head")),
        check_vma=False,
    )
```

```python
import jax
import jax.numpy as jnp
from jax import lax
from jax.experimental import pallas as pl
from jax.sharding import PartitionSpec as P

D = 2048
HD = 128
BLK = 128
REACH = 3
WIN = 6


NEG_FILL = -1e30
NORM_EPS = 1e-06


def from_behind(block, axis, distance):
    devices = range(lax.axis_size(axis))
    route = [(i - distance, i) for i in devices if i - distance in devices]
    return lax.ppermute(block, axis, route)


def chip_swap(block, axis):
    size = lax.axis_size(axis)
    return lax.ppermute(block, axis, [(i, i ^ 1) for i in range(size)])


def all_sum(block, axis):
    size = lax.axis_size(axis)
    if size & (size - 1):
        return lax.psum(block, axis)
    stride = 1
    while stride < size:
        block = block + lax.ppermute(block, axis, [(i, i ^ stride) for i in range(size)])
        stride *= 2
    return block


def pair_sum(block, axis):
    if lax.axis_size(axis) != 2:
        return lax.psum(block, axis)
    return block + lax.ppermute(block, axis, [(0, 1), (1, 0)])


def split_heads(array):
    return array.reshape(array.shape[0], array.shape[1] // HD, HD)


def _scores(q_ref, k_ref, allowed_ref):
    raw = lax.dot_general(
        q_ref[...], k_ref[...], (((1,), (1,)), ((), ())), preferred_element_type=jnp.float32
    ) * (HD ** (-0.5))
    allowed = allowed_ref[...] > 0
    return jnp.where(allowed, raw, NEG_FILL), allowed


def _forward_kernel(q_ref, k_ref, v_ref, allowed_ref, out_ref, peak_ref, total_ref):
    scores, allowed = _scores(q_ref, k_ref, allowed_ref)
    peak = jnp.max(scores, axis=1, keepdims=True)
    expo = jnp.where(allowed, jnp.exp(scores - peak), 0.0)
    total = jnp.sum(expo, axis=1, keepdims=True)
    weights = (expo / total).astype(jnp.bfloat16)
    out_ref[...] = jnp.dot(weights, v_ref[...], preferred_element_type=jnp.float32)
    peak_ref[...] = jnp.broadcast_to(peak, peak_ref.shape)
    total_ref[...] = jnp.broadcast_to(total, total_ref.shape)


def _backward_kernel(q_ref, k_ref, v_ref, allowed_ref, g_ref, peak_ref, total_ref, delta_ref,
                     dq_ref, dk_ref, dv_ref):
    scores, allowed = _scores(q_ref, k_ref, allowed_ref)
    expo = jnp.where(allowed, jnp.exp(scores - peak_ref[:, :1]), 0.0)
    prob = expo / total_ref[:, :1]
    grad = g_ref[...]
    prob_grad = lax.dot_general(
        grad, v_ref[...], (((1,), (1,)), ((), ())), preferred_element_type=jnp.float32
    )
    score_grad = (prob * (prob_grad - delta_ref[:, :1])).astype(jnp.bfloat16)
    scale = HD ** (-0.5)
    dq_ref[...] = jnp.dot(score_grad, k_ref[...], preferred_element_type=jnp.float32) * scale
    dk_ref[...] = lax.dot_general(
        score_grad, q_ref[...], (((0,), (0,)), ((), ())), preferred_element_type=jnp.float32
    ) * scale
    dv_ref[...] = lax.dot_general(
        prob.astype(jnp.bfloat16), grad, (((0,), (0,)), ((), ())), preferred_element_type=jnp.float32
    )


def _head_spec(rows):
    return pl.BlockSpec((rows, HD), lambda h: (0, h))


def attention_forward(queries, key_win, value_win, allowed, interpret=False):
    rows, channels = queries.shape
    keys_n = key_win.shape[0]
    heads = channels // HD
    return pl.pallas_call(
        _forward_kernel,
        grid=(heads,),
        in_specs=[_head_spec(rows), _head_spec(keys_n), _head_spec(keys_n),
                  pl.BlockSpec((rows, keys_n), lambda h: (0, 0))],
        out_specs=[_head_spec(rows), _head_spec(rows), _head_spec(rows)],
        out_shape=[jax.ShapeDtypeStruct((rows, channels), jnp.float32)] * 3,
        interpret=interpret,
    )(queries, key_win, value_win, allowed)


def attention_backward(queries, key_win, value_win, allowed, grad, peak, total, delta, interpret=False):
    rows, channels = queries.shape
    keys_n = key_win.shape[0]
    heads = channels // HD
    return pl.pallas_call(
        _backward_kernel,
        grid=(heads,),
        in_specs=[_head_spec(rows), _head_spec(keys_n), _head_spec(keys_n),
                  pl.BlockSpec((rows, keys_n), lambda h: (0, 0)),
                  _head_spec(rows), _head_spec(rows), _head_spec(rows), _head_spec(rows)],
        out_specs=[_head_spec(rows), _head_spec(keys_n), _head_spec(keys_n)],
        out_shape=[jax.ShapeDtypeStruct((rows, channels), jnp.float32),
                   jax.ShapeDtypeStruct((keys_n, channels), jnp.float32),
                   jax.ShapeDtypeStruct((keys_n, channels), jnp.float32)],
        interpret=interpret,
    )(queries, key_win, value_win, allowed, grad, peak, total, delta)


def window_mask(block_bits, device, row_count, key_count):
    per_device = row_count // BLK
    key_blocks = key_count // BLK
    first_block = device * per_device - (key_blocks - per_device)
    qb = jnp.arange(per_device, dtype=jnp.int32)
    kb = jnp.arange(key_blocks, dtype=jnp.int32)
    relative = qb[:, None] + (key_blocks - per_device) - kb[None, :]
    one_hot = relative[:, :, None] == jnp.arange(WIN, dtype=jnp.int32)[None, None, :]
    picked_bits = jnp.sum(jnp.where(one_hot, block_bits[:, None, :], 0), axis=2)
    coarse = (picked_bits > 0) & (relative >= 0) & (relative < WIN) & (first_block + kb[None, :] >= 0)
    fine = jnp.repeat(jnp.repeat(coarse, BLK, axis=0), BLK, axis=1)
    q = jnp.arange(row_count, dtype=jnp.int32)
    s = jnp.arange(key_count, dtype=jnp.int32)
    causal = s[None, :] <= q[:, None] + (key_count - row_count)
    return fine & causal


def body(queries, keys, values_in, teacher, gain, conv_weight, block_bits, mask_pos):
    row_count, channels = queries.shape
    tap_count = conv_weight.shape[0]
    rim_rows = tap_count - 1
    device = lax.axis_index("tm")
    even = device % 2 == 0
    score_scale = HD ** (-0.5)
    far_rows = row_count - BLK
    far_lead = 8
    key_count = REACH * row_count + (row_count - far_rows)

    def relay(own):
        second = from_behind(own, "tm", 2)
        first = chip_swap(jnp.where(even, own, second), "tm")
        third = from_behind(second[far_rows - far_lead :], "tm", 1)
        return jnp.concatenate([third, second, first, own], 0)

    key_win = relay(keys)[far_lead:]
    vin_win = relay(values_in).astype(jnp.float32)

    conv_sum = jnp.zeros((key_count, channels), jnp.float32)
    for tap_index in range(tap_count):
        conv_sum = conv_sum + conv_weight[tap_index] * vin_win[far_lead - tap_index : far_lead - tap_index + key_count]
    value_win = conv_sum.astype(jnp.bfloat16)

    allowed = window_mask(block_bits, device, row_count, key_count).astype(jnp.float32)
    flattened, row_peak, row_total = attention_forward(queries, key_win, value_win, allowed)

    squares = pair_sum(jnp.sum(flattened * flattened, axis=1), "head")
    inverse = lax.rsqrt(squares / D + NORM_EPS)
    prediction = flattened * inverse[:, None] * gain
    position = jnp.arange(row_count, dtype=jnp.int32) % BLK
    chosen = jnp.any(jnp.repeat(mask_pos, BLK, axis=0) == position[:, None], axis=1)
    residual = jnp.where(chosen[:, None], prediction - teacher.astype(jnp.float32), 0.0)
    scaled = residual * gain
    cross_term = pair_sum(jnp.sum(scaled * flattened, axis=1), "head")
    out_grad = (
        inverse[:, None] * scaled - flattened * (inverse**3 * cross_term / D)[:, None]
    ).astype(jnp.bfloat16)
    grad_f = out_grad.astype(jnp.float32)
    delta = jnp.sum(split_heads(grad_f * flattened), axis=2)
    delta_wide = jnp.repeat(delta, HD, axis=1)
    query_grad, key_part, value_part = attention_backward(
        queries, key_win, value_win, allowed, out_grad, row_peak, row_total, delta_wide
    )

    local_taps = jnp.stack(
        [
            jnp.sum(value_part * vin_win[far_lead - tap_index : far_lead - tap_index + key_count], axis=0)
            for tap_index in range(tap_count)
        ]
    )
    conv_grad = all_sum(local_taps, "tm")

    lead = jnp.zeros((far_lead, channels), jnp.float32)
    padded_value = jnp.concatenate([lead, value_part, jnp.zeros((rim_rows, channels), jnp.float32)], 0)
    value_sum = jnp.zeros((key_count + far_lead, channels), jnp.float32)
    for tap_index in range(tap_count):
        value_sum = value_sum + conv_weight[tap_index] * padded_value[tap_index : tap_index + key_count + far_lead]

    def relay_back(grads):
        cut_third = row_count - far_rows + far_lead
        grad_third = grads[:cut_third]
        grad_second = grads[cut_third : cut_third + row_count]
        grad_first = grads[cut_third + row_count : cut_third + 2 * row_count]
        grad_own = grads[cut_third + 2 * row_count :]
        back_third = from_behind(grad_third.astype(jnp.bfloat16), "tm", -1).astype(jnp.float32)
        back_first = chip_swap(grad_first.astype(jnp.bfloat16), "tm").astype(jnp.float32)
        grad_second = grad_second + jnp.concatenate(
            [jnp.zeros((far_rows - far_lead, grads.shape[1]), jnp.float32), back_third], 0
        )
        grad_second = grad_second + jnp.where(even, 0.0, back_first)
        back_second = from_behind(grad_second.astype(jnp.bfloat16), "tm", -2).astype(jnp.float32)
        return grad_own + jnp.where(even, back_first, 0.0) + back_second

    value_total = relay_back(value_sum)
    key_total = relay_back(jnp.concatenate([lead, key_part], 0))

    return (
        query_grad.astype(jnp.bfloat16),
        key_total.astype(jnp.bfloat16),
        value_total.astype(jnp.bfloat16),
        conv_grad,
    )


def solution(mesh):
    placed = (
        P("tm", "head"),
        P("tm", "head"),
        P("tm", "head"),
        P("tm", "head"),
        P("head"),
        P(None, "head"),
        P("tm", None),
        P("tm", None),
    )
    return jax.shard_map(
        body,
        mesh=mesh,
        in_specs=placed,
        out_specs=(P("tm", "head"), P("tm", "head"), P("tm", "head"), P(None, "head")),
        check_vma=False,
    )
```

```python
import jax
import jax.numpy as jnp
from jax import lax
from jax.experimental import pallas as pl
from jax.sharding import PartitionSpec as P

D = 2048
HD = 128
BLK = 128
REACH = 3
WIN = 6


NEG_FILL = -1e30
NORM_EPS = 1e-06


def from_behind(block, axis, distance):
    devices = range(lax.axis_size(axis))
    route = [(i - distance, i) for i in devices if i - distance in devices]
    return lax.ppermute(block, axis, route)


def chip_swap(block, axis):
    size = lax.axis_size(axis)
    return lax.ppermute(block, axis, [(i, i ^ 1) for i in range(size)])


def all_sum(block, axis):
    size = lax.axis_size(axis)
    if size & (size - 1):
        return lax.psum(block, axis)
    stride = 1
    while stride < size:
        block = block + lax.ppermute(block, axis, [(i, i ^ stride) for i in range(size)])
        stride *= 2
    return block


def pair_sum(block, axis):
    if lax.axis_size(axis) != 2:
        return lax.psum(block, axis)
    return block + lax.ppermute(block, axis, [(0, 1), (1, 0)])


def split_heads(array):
    return array.reshape(array.shape[0], array.shape[1] // HD, HD)


def _scores(q_ref, k_ref, allowed_ref):
    raw = lax.dot_general(
        q_ref[...], k_ref[...], (((1,), (1,)), ((), ())), preferred_element_type=jnp.float32
    ) * (HD ** (-0.5))
    allowed = allowed_ref[...] > 0
    return jnp.where(allowed, raw, NEG_FILL), allowed


def _forward_kernel(q_ref, k_ref, v_ref, vin_ref, allowed_ref, out_ref, peak_ref, total_ref, mixed_ref):
    scores, allowed = _scores(q_ref, k_ref, allowed_ref)
    peak = jnp.max(scores, axis=1, keepdims=True)
    expo = jnp.where(allowed, jnp.exp(scores - peak), 0.0)
    total = jnp.sum(expo, axis=1, keepdims=True)
    weights = (expo / total).astype(jnp.bfloat16)
    out_ref[...] = jnp.dot(weights, v_ref[...], preferred_element_type=jnp.float32)
    peak_ref[...] = jnp.broadcast_to(peak, peak_ref.shape)
    total_ref[...] = jnp.broadcast_to(total, total_ref.shape)
    keys_n = k_ref.shape[0]
    lead = vin_ref.shape[0] - keys_n
    for tap_index in range(mixed_ref.shape[0]):
        shifted = vin_ref[lead - tap_index : lead - tap_index + keys_n, :].astype(jnp.bfloat16)
        mixed_ref[tap_index] = jnp.dot(weights, shifted, preferred_element_type=jnp.float32)


def _probabilities(q_ref, k_ref, allowed_ref, peak_ref, total_ref):
    scores, allowed = _scores(q_ref, k_ref, allowed_ref)
    expo = jnp.where(allowed, jnp.exp(scores - peak_ref[:, :1]), 0.0)
    return expo / total_ref[:, :1]


def _value_grad_kernel(q_ref, k_ref, allowed_ref, g_ref, peak_ref, total_ref, dv_ref):
    prob = _probabilities(q_ref, k_ref, allowed_ref, peak_ref, total_ref)
    dv_ref[...] = lax.dot_general(
        prob.astype(jnp.bfloat16), g_ref[...], (((0,), (0,)), ((), ())), preferred_element_type=jnp.float32
    )


def _backward_kernel(q_ref, k_ref, v_ref, allowed_ref, g_ref, peak_ref, total_ref, att_ref,
                     dq_ref, dk_ref):
    prob = _probabilities(q_ref, k_ref, allowed_ref, peak_ref, total_ref)
    grad = g_ref[...]
    delta = jnp.sum(grad.astype(jnp.float32) * att_ref[...], axis=1, keepdims=True)
    prob_grad = lax.dot_general(
        grad, v_ref[...], (((1,), (1,)), ((), ())), preferred_element_type=jnp.float32
    )
    score_grad = (prob * (prob_grad - delta)).astype(jnp.bfloat16)
    scale = HD ** (-0.5)
    dq_ref[...] = jnp.dot(score_grad, k_ref[...], preferred_element_type=jnp.float32) * scale
    dk_ref[...] = lax.dot_general(
        score_grad, q_ref[...], (((0,), (0,)), ((), ())), preferred_element_type=jnp.float32
    ) * scale


def _head_spec(rows):
    return pl.BlockSpec((rows, HD), lambda h: (0, h))


def attention_forward(queries, key_win, value_win, vin_win, allowed, taps, interpret=False):
    rows, channels = queries.shape
    keys_n = key_win.shape[0]
    heads = channels // HD
    return pl.pallas_call(
        _forward_kernel,
        grid=(heads,),
        in_specs=[_head_spec(rows), _head_spec(keys_n), _head_spec(keys_n), _head_spec(vin_win.shape[0]),
                  pl.BlockSpec((rows, keys_n), lambda h: (0, 0))],
        out_specs=[_head_spec(rows), _head_spec(rows), _head_spec(rows),
                   pl.BlockSpec((taps, rows, HD), lambda h: (0, 0, h))],
        out_shape=[jax.ShapeDtypeStruct((rows, channels), jnp.float32)] * 3
        + [jax.ShapeDtypeStruct((taps, rows, channels), jnp.float32)],
        interpret=interpret,
    )(queries, key_win, value_win, vin_win, allowed)


def value_grad(queries, key_win, allowed, grad, peak, total, interpret=False):
    rows, channels = queries.shape
    keys_n = key_win.shape[0]
    return pl.pallas_call(
        _value_grad_kernel,
        grid=(channels // HD,),
        in_specs=[_head_spec(rows), _head_spec(keys_n), pl.BlockSpec((rows, keys_n), lambda h: (0, 0)),
                  _head_spec(rows), _head_spec(rows), _head_spec(rows)],
        out_specs=_head_spec(keys_n),
        out_shape=jax.ShapeDtypeStruct((keys_n, channels), jnp.float32),
        interpret=interpret,
    )(queries, key_win, allowed, grad, peak, total)


def attention_backward(queries, key_win, value_win, allowed, grad, peak, total, attended, interpret=False):
    rows, channels = queries.shape
    keys_n = key_win.shape[0]
    heads = channels // HD
    return pl.pallas_call(
        _backward_kernel,
        grid=(heads,),
        in_specs=[_head_spec(rows), _head_spec(keys_n), _head_spec(keys_n),
                  pl.BlockSpec((rows, keys_n), lambda h: (0, 0)),
                  _head_spec(rows), _head_spec(rows), _head_spec(rows), _head_spec(rows)],
        out_specs=[_head_spec(rows), _head_spec(keys_n)],
        out_shape=[jax.ShapeDtypeStruct((rows, channels), jnp.float32),
                   jax.ShapeDtypeStruct((keys_n, channels), jnp.float32)],
        interpret=interpret,
    )(queries, key_win, value_win, allowed, grad, peak, total, attended)


def window_mask(block_bits, device, row_count, key_count):
    per_device = row_count // BLK
    key_blocks = key_count // BLK
    first_block = device * per_device - (key_blocks - per_device)
    qb = jnp.arange(per_device, dtype=jnp.int32)
    kb = jnp.arange(key_blocks, dtype=jnp.int32)
    relative = qb[:, None] + (key_blocks - per_device) - kb[None, :]
    one_hot = relative[:, :, None] == jnp.arange(WIN, dtype=jnp.int32)[None, None, :]
    picked_bits = jnp.sum(jnp.where(one_hot, block_bits[:, None, :], 0), axis=2)
    coarse = (picked_bits > 0) & (relative >= 0) & (relative < WIN) & (first_block + kb[None, :] >= 0)
    fine = jnp.repeat(jnp.repeat(coarse, BLK, axis=0), BLK, axis=1)
    q = jnp.arange(row_count, dtype=jnp.int32)
    s = jnp.arange(key_count, dtype=jnp.int32)
    causal = s[None, :] <= q[:, None] + (key_count - row_count)
    return fine & causal


def body(queries, keys, values_in, teacher, gain, conv_weight, block_bits, mask_pos):
    row_count, channels = queries.shape
    tap_count = conv_weight.shape[0]
    rim_rows = tap_count - 1
    device = lax.axis_index("tm")
    even = device % 2 == 0
    score_scale = HD ** (-0.5)
    far_rows = row_count - BLK
    far_lead = 8
    key_count = REACH * row_count + (row_count - far_rows)

    def relay(own):
        second = from_behind(own, "tm", 2)
        first = chip_swap(jnp.where(even, own, second), "tm")
        third = from_behind(second[far_rows - far_lead :], "tm", 1)
        return jnp.concatenate([third, second, first, own], 0)

    key_win = relay(keys)[far_lead:]
    vin_win = relay(values_in).astype(jnp.float32)

    conv_sum = jnp.zeros((key_count, channels), jnp.float32)
    for tap_index in range(tap_count):
        conv_sum = conv_sum + conv_weight[tap_index] * vin_win[far_lead - tap_index : far_lead - tap_index + key_count]
    value_win = conv_sum.astype(jnp.bfloat16)

    allowed = window_mask(block_bits, device, row_count, key_count).astype(jnp.float32)
    flattened, row_peak, row_total, mixed = attention_forward(
        queries, key_win, value_win, vin_win, allowed, tap_count
    )

    squares = pair_sum(jnp.sum(flattened * flattened, axis=1), "head")
    inverse = lax.rsqrt(squares / D + NORM_EPS)
    prediction = flattened * inverse[:, None] * gain
    position = jnp.arange(row_count, dtype=jnp.int32) % BLK
    chosen = jnp.any(jnp.repeat(mask_pos, BLK, axis=0) == position[:, None], axis=1)
    residual = jnp.where(chosen[:, None], prediction - teacher.astype(jnp.float32), 0.0)
    scaled = residual * gain
    cross_term = pair_sum(jnp.sum(scaled * flattened, axis=1), "head")
    out_grad = (
        inverse[:, None] * scaled - flattened * (inverse**3 * cross_term / D)[:, None]
    ).astype(jnp.bfloat16)
    value_part = value_grad(queries, key_win, allowed, out_grad, row_peak, row_total)
    query_grad, key_part = attention_backward(
        queries, key_win, value_win, allowed, out_grad, row_peak, row_total, flattened
    )

    local_taps = jnp.sum(out_grad.astype(jnp.float32)[None] * mixed, axis=1)
    conv_grad = all_sum(local_taps, "tm")

    lead = jnp.zeros((far_lead, channels), jnp.float32)
    padded_value = jnp.concatenate([lead, value_part, jnp.zeros((rim_rows, channels), jnp.float32)], 0)
    value_sum = jnp.zeros((key_count + far_lead, channels), jnp.float32)
    for tap_index in range(tap_count):
        value_sum = value_sum + conv_weight[tap_index] * padded_value[tap_index : tap_index + key_count + far_lead]

    def relay_back(grads):
        cut_third = row_count - far_rows + far_lead
        grad_third = grads[:cut_third]
        grad_second = grads[cut_third : cut_third + row_count]
        grad_first = grads[cut_third + row_count : cut_third + 2 * row_count]
        grad_own = grads[cut_third + 2 * row_count :]
        back_third = from_behind(grad_third.astype(jnp.bfloat16), "tm", -1).astype(jnp.float32)
        back_first = chip_swap(grad_first.astype(jnp.bfloat16), "tm").astype(jnp.float32)
        grad_second = grad_second + jnp.concatenate(
            [jnp.zeros((far_rows - far_lead, grads.shape[1]), jnp.float32), back_third], 0
        )
        grad_second = grad_second + jnp.where(even, 0.0, back_first)
        back_second = from_behind(grad_second.astype(jnp.bfloat16), "tm", -2).astype(jnp.float32)
        return grad_own + jnp.where(even, back_first, 0.0) + back_second

    value_total = relay_back(value_sum)
    key_total = relay_back(jnp.concatenate([lead, key_part], 0))

    return (
        query_grad.astype(jnp.bfloat16),
        key_total.astype(jnp.bfloat16),
        value_total.astype(jnp.bfloat16),
        conv_grad,
    )


def solution(mesh):
    placed = (
        P("tm", "head"),
        P("tm", "head"),
        P("tm", "head"),
        P("tm", "head"),
        P("head"),
        P(None, "head"),
        P("tm", None),
        P("tm", None),
    )
    return jax.shard_map(
        body,
        mesh=mesh,
        in_specs=placed,
        out_specs=(P("tm", "head"), P("tm", "head"), P("tm", "head"), P(None, "head")),
        check_vma=False,
    )
```

```python
import jax
import jax.numpy as jnp
from jax import lax
from jax.sharding import PartitionSpec as P

D = 2048
HD = 128
BLK = 128
REACH = 3
WIN = 6


NEG_FILL = -1e30
NORM_EPS = 1e-06


def from_behind(block, axis, distance):
    devices = range(lax.axis_size(axis))
    route = [(i - distance, i) for i in devices if i - distance in devices]
    return lax.ppermute(block, axis, route)


def chip_swap(block, axis):
    size = lax.axis_size(axis)
    return lax.ppermute(block, axis, [(i, i ^ 1) for i in range(size)])


def all_sum(block, axis):
    size = lax.axis_size(axis)
    if size & (size - 1):
        return lax.psum(block, axis)
    stride = size // 2
    while stride >= 1:
        block = block + lax.ppermute(block, axis, [(i, i ^ stride) for i in range(size)])
        stride //= 2
    return block


def pair_sum(block, axis):
    if lax.axis_size(axis) != 2:
        return lax.psum(block, axis)
    return block + lax.ppermute(block, axis, [(0, 1), (1, 0)])


def split_heads(array):
    return array.reshape(array.shape[0], array.shape[1] // HD, HD)


def window_mask(block_bits, device, row_count, key_count):
    per_device = row_count // BLK
    key_blocks = key_count // BLK
    first_block = device * per_device - (key_blocks - per_device)
    qb = jnp.arange(per_device, dtype=jnp.int32)
    kb = jnp.arange(key_blocks, dtype=jnp.int32)
    relative = qb[:, None] + (key_blocks - per_device) - kb[None, :]
    one_hot = relative[:, :, None] == jnp.arange(WIN, dtype=jnp.int32)[None, None, :]
    picked_bits = jnp.sum(jnp.where(one_hot, block_bits[:, None, :], 0), axis=2)
    coarse = (picked_bits > 0) & (relative >= 0) & (relative < WIN) & (first_block + kb[None, :] >= 0)
    fine = jnp.repeat(jnp.repeat(coarse, BLK, axis=0), BLK, axis=1)
    q = jnp.arange(row_count, dtype=jnp.int32)
    s = jnp.arange(key_count, dtype=jnp.int32)
    causal = s[None, :] <= q[:, None] + (key_count - row_count)
    return fine & causal


def body(queries, keys, values_in, teacher, gain, conv_weight, block_bits, mask_pos):
    row_count, channels = queries.shape
    tap_count = conv_weight.shape[0]
    rim_rows = tap_count - 1
    device = lax.axis_index("tm")
    even = device % 2 == 0
    score_scale = HD ** (-0.5)
    far_rows = row_count - BLK
    far_lead = 8
    key_count = REACH * row_count + (row_count - far_rows)

    def relay(own):
        second = from_behind(own, "tm", 2)
        first = chip_swap(jnp.where(even, own, second), "tm")
        third = from_behind(second[far_rows - far_lead :], "tm", 1)
        return jnp.concatenate([third, second, first, own], 0)

    key_win = relay(keys)[far_lead:]
    vin_win = relay(values_in)

    conv_sum = jnp.zeros((key_count, channels), jnp.float32)
    for tap_index in range(tap_count):
        conv_sum = conv_sum + conv_weight[tap_index] * vin_win[
            far_lead - tap_index : far_lead - tap_index + key_count
        ].astype(jnp.float32)
    value_win = conv_sum.astype(jnp.bfloat16)

    heads_query = split_heads(queries)
    heads_key = split_heads(key_win)
    heads_value = split_heads(value_win)
    mask = window_mask(block_bits, device, row_count, key_count)

    raw_scores = (
        jnp.einsum("thd,uhd->htu", heads_query, heads_key, preferred_element_type=jnp.float32)
        * score_scale
    )
    scores = jnp.where(mask[None], raw_scores, NEG_FILL)
    row_peak = jnp.max(scores, axis=2)
    expo = jnp.where(mask[None], jnp.exp(scores - row_peak[..., None]), 0.0)
    row_total = jnp.sum(expo, axis=2)
    prob = expo / row_total[..., None]
    weights = prob.astype(jnp.bfloat16)
    attended = jnp.einsum("htu,uhd->thd", weights, heads_value, preferred_element_type=jnp.float32)

    flattened = attended.reshape(row_count, channels)
    position = jnp.arange(row_count, dtype=jnp.int32) % BLK
    chosen = jnp.any(jnp.repeat(mask_pos, BLK, axis=0) == position[:, None], axis=1)
    weighted = flattened * gain
    sums = pair_sum(
        jnp.stack(
            [
                jnp.sum(flattened * flattened, axis=1),
                jnp.sum(weighted * weighted, axis=1),
                jnp.sum(teacher.astype(jnp.float32) * weighted, axis=1),
            ]
        ),
        "head",
    )
    squares = sums[0]
    inverse = lax.rsqrt(squares / D + NORM_EPS)
    prediction = flattened * inverse[:, None] * gain
    residual = jnp.where(chosen[:, None], prediction - teacher.astype(jnp.float32), 0.0)
    scaled = residual * gain
    cross_term = jnp.where(chosen, inverse * sums[1] - sums[2], 0.0)
    out_grad = (
        inverse[:, None] * scaled - flattened * (inverse**3 * cross_term / D)[:, None]
    ).astype(jnp.bfloat16)
    heads_grad = split_heads(out_grad)
    delta = jnp.sum(heads_grad.astype(jnp.float32) * attended, axis=2).T

    prob_grad = jnp.einsum("thd,uhd->htu", heads_grad, heads_value, preferred_element_type=jnp.float32)
    score_grad = (prob * (prob_grad - delta[:, :, None])).astype(jnp.bfloat16)
    query_grad = (
        jnp.einsum("htu,uhd->thd", score_grad, heads_key, preferred_element_type=jnp.float32)
        * score_scale
    )
    key_part = (
        jnp.einsum("htu,thd->uhd", score_grad, heads_query, preferred_element_type=jnp.float32)
        * score_scale
    ).reshape(key_count, channels)
    value_part = jnp.einsum(
        "htu,thd->uhd", weights, heads_grad, preferred_element_type=jnp.float32
    ).reshape(key_count, channels)

    local_taps = jnp.stack(
        [
            jnp.sum(
                value_part
                * vin_win[far_lead - tap_index : far_lead - tap_index + key_count].astype(jnp.float32),
                axis=0,
            )
            for tap_index in range(tap_count)
        ]
    )
    conv_grad = all_sum(local_taps, "tm")

    lead = jnp.zeros((far_lead, channels), jnp.float32)
    padded_value = jnp.concatenate([lead, value_part, jnp.zeros((rim_rows, channels), jnp.float32)], 0)
    value_sum = jnp.zeros((key_count + far_lead, channels), jnp.float32)
    for tap_index in range(tap_count):
        value_sum = value_sum + conv_weight[tap_index] * padded_value[tap_index : tap_index + key_count + far_lead]

    def relay_back(grads):
        cut_third = row_count - far_rows + far_lead
        grad_third = grads[:cut_third]
        grad_second = grads[cut_third : cut_third + row_count]
        grad_first = grads[cut_third + row_count : cut_third + 2 * row_count]
        grad_own = grads[cut_third + 2 * row_count :]
        back_third = from_behind(grad_third.astype(jnp.bfloat16), "tm", -1).astype(jnp.float32)
        back_first = chip_swap(grad_first.astype(jnp.bfloat16), "tm").astype(jnp.float32)
        grad_second = grad_second + jnp.concatenate(
            [jnp.zeros((far_rows - far_lead, grads.shape[1]), jnp.float32), back_third], 0
        )
        grad_second = grad_second + jnp.where(even, 0.0, back_first)
        back_second = from_behind(grad_second.astype(jnp.bfloat16), "tm", -2).astype(jnp.float32)
        return grad_own + jnp.where(even, back_first, 0.0) + back_second

    value_total = relay_back(value_sum)
    key_total = relay_back(jnp.concatenate([lead, key_part], 0))

    return (
        query_grad.reshape(row_count, channels).astype(jnp.bfloat16),
        key_total.astype(jnp.bfloat16),
        value_total.astype(jnp.bfloat16),
        conv_grad,
    )


def solution(mesh):
    placed = (
        P("tm", "head"),
        P("tm", "head"),
        P("tm", "head"),
        P("tm", "head"),
        P("head"),
        P(None, "head"),
        P("tm", None),
        P("tm", None),
    )
    return jax.shard_map(
        body,
        mesh=mesh,
        in_specs=placed,
        out_specs=(P("tm", "head"), P("tm", "head"), P("tm", "head"), P(None, "head")),
        check_vma=False,
    )
```

```python
import jax
import jax.numpy as jnp
from jax import lax
from jax.sharding import PartitionSpec as P

D = 2048
HD = 128
BLK = 128
REACH = 3
WIN = 6


NEG_FILL = -1e30
NORM_EPS = 1e-06


def from_behind(block, axis, distance):
    devices = range(lax.axis_size(axis))
    route = [(i - distance, i) for i in devices if i - distance in devices]
    return lax.ppermute(block, axis, route)


def chip_swap(block, axis):
    size = lax.axis_size(axis)
    return lax.ppermute(block, axis, [(i, i ^ 1) for i in range(size)])


def all_sum(block, axis):
    size = lax.axis_size(axis)
    if size & (size - 1):
        return lax.psum(block, axis)
    stride = 1
    while stride < size:
        block = block + lax.ppermute(block, axis, [(i, i ^ stride) for i in range(size)])
        stride *= 2
    return block


def pair_sum(block, axis):
    if lax.axis_size(axis) != 2:
        return lax.psum(block, axis)
    return block + lax.ppermute(block, axis, [(0, 1), (1, 0)])


def split_heads(array):
    return array.reshape(array.shape[0], array.shape[1] // HD, HD)


def window_mask(block_bits, device, row_count, key_count):
    per_device = row_count // BLK
    key_blocks = key_count // BLK
    first_block = device * per_device - (key_blocks - per_device)
    qb = jnp.arange(per_device, dtype=jnp.int32)
    kb = jnp.arange(key_blocks, dtype=jnp.int32)
    relative = qb[:, None] + (key_blocks - per_device) - kb[None, :]
    one_hot = relative[:, :, None] == jnp.arange(WIN, dtype=jnp.int32)[None, None, :]
    picked_bits = jnp.sum(jnp.where(one_hot, block_bits[:, None, :], 0), axis=2)
    coarse = (picked_bits > 0) & (relative >= 0) & (relative < WIN) & (first_block + kb[None, :] >= 0)
    fine = jnp.repeat(jnp.repeat(coarse, BLK, axis=0), BLK, axis=1)
    q = jnp.arange(row_count, dtype=jnp.int32)
    s = jnp.arange(key_count, dtype=jnp.int32)
    causal = s[None, :] <= q[:, None] + (key_count - row_count)
    return fine & causal


def body(queries, keys, values_in, teacher, gain, conv_weight, block_bits, mask_pos):
    row_count, channels = queries.shape
    tap_count = conv_weight.shape[0]
    rim_rows = tap_count - 1
    device = lax.axis_index("tm")
    even = device % 2 == 0
    score_scale = HD ** (-0.5)
    far_rows = row_count - BLK
    far_lead = 8
    key_count = REACH * row_count + (row_count - far_rows)

    def relay(own):
        second = from_behind(own, "tm", 2)
        first = chip_swap(jnp.where(even, own, second), "tm")
        third = from_behind(second[far_rows - far_lead :], "tm", 1)
        return jnp.concatenate([third, second, first, own], 0)

    key_win = relay(keys)[far_lead:]
    vin_win = relay(values_in)

    conv_sum = jnp.zeros((key_count, channels), jnp.float32)
    for tap_index in range(tap_count):
        conv_sum = conv_sum + conv_weight[tap_index] * vin_win[
            far_lead - tap_index : far_lead - tap_index + key_count
        ].astype(jnp.float32)
    value_win = conv_sum.astype(jnp.bfloat16)

    heads_query = split_heads(queries)
    heads_key = split_heads(key_win)
    heads_value = split_heads(value_win)
    mask = window_mask(block_bits, device, row_count, key_count)

    raw_scores = (
        jnp.einsum("thd,uhd->htu", heads_query, heads_key, preferred_element_type=jnp.float32)
        * score_scale
    )
    scores = jnp.where(mask[None], raw_scores, NEG_FILL)
    row_peak = jnp.max(scores, axis=2)
    expo = jnp.where(mask[None], jnp.exp(scores - row_peak[..., None]), 0.0)
    row_total = jnp.sum(expo, axis=2)
    prob = expo / row_total[..., None]
    weights = prob.astype(jnp.bfloat16)
    attended = jnp.einsum("htu,uhd->thd", weights, heads_value, preferred_element_type=jnp.float32)

    flattened = attended.reshape(row_count, channels)
    position = jnp.arange(row_count, dtype=jnp.int32) % BLK
    chosen = jnp.any(jnp.repeat(mask_pos, BLK, axis=0) == position[:, None], axis=1)
    weighted = flattened * gain
    sums = pair_sum(
        jnp.stack(
            [
                jnp.sum(flattened * flattened, axis=1),
                jnp.sum(weighted * weighted, axis=1),
                jnp.sum(teacher.astype(jnp.float32) * weighted, axis=1),
            ]
        ),
        "head",
    )
    squares = sums[0]
    inverse = lax.rsqrt(squares / D + NORM_EPS)
    prediction = flattened * inverse[:, None] * gain
    residual = jnp.where(chosen[:, None], prediction - teacher.astype(jnp.float32), 0.0)
    scaled = residual * gain
    cross_term = jnp.where(chosen, inverse * sums[1] - sums[2], 0.0)
    out_grad = (
        inverse[:, None] * scaled - flattened * (inverse**3 * cross_term / D)[:, None]
    ).astype(jnp.bfloat16)
    heads_grad = split_heads(out_grad)
    delta = jnp.sum(heads_grad.astype(jnp.float32) * attended, axis=2).T

    prob_grad = jnp.einsum("thd,uhd->htu", heads_grad, heads_value, preferred_element_type=jnp.float32)
    score_grad = (prob * (prob_grad - delta[:, :, None])).astype(jnp.bfloat16)
    query_grad = (
        jnp.einsum("htu,uhd->thd", score_grad, heads_key, preferred_element_type=jnp.float32)
        * score_scale
    )
    key_part = (
        jnp.einsum("htu,thd->uhd", score_grad, heads_query, preferred_element_type=jnp.float32)
        * score_scale
    ).reshape(key_count, channels)
    value_part = jnp.einsum(
        "htu,thd->uhd", weights, heads_grad, preferred_element_type=jnp.float32
    ).reshape(key_count, channels)

    local_taps = jnp.stack(
        [
            jnp.sum(
                value_part
                * vin_win[far_lead - tap_index : far_lead - tap_index + key_count].astype(jnp.float32),
                axis=0,
            )
            for tap_index in range(tap_count)
        ]
    )
    conv_grad = all_sum(local_taps, "tm")

    lead = jnp.zeros((far_lead, channels), jnp.float32)
    padded_value = jnp.concatenate([lead, value_part, jnp.zeros((rim_rows, channels), jnp.float32)], 0)
    value_sum = jnp.zeros((key_count + far_lead, channels), jnp.float32)
    for tap_index in range(tap_count):
        value_sum = value_sum + conv_weight[tap_index] * padded_value[tap_index : tap_index + key_count + far_lead]

    def send_back(grads):
        cut_third = row_count - far_rows + far_lead
        grad_third = grads[:cut_third]
        grad_second = grads[cut_third : cut_third + row_count]
        grad_first = grads[cut_third + row_count : cut_third + 2 * row_count]
        grad_own = grads[cut_third + 2 * row_count :]
        back = [
            from_behind(part.astype(jnp.bfloat16), "tm", -distance).astype(jnp.float32)
            for distance, part in ((1, grad_first), (2, grad_second), (3, grad_third))
        ]
        far = jnp.concatenate([jnp.zeros((far_rows - far_lead, grads.shape[1]), jnp.float32), back[2]], 0)
        return grad_own + back[0] + back[1] + far

    value_total = send_back(value_sum)
    key_total = send_back(jnp.concatenate([lead, key_part], 0))

    return (
        query_grad.reshape(row_count, channels).astype(jnp.bfloat16),
        key_total.astype(jnp.bfloat16),
        value_total.astype(jnp.bfloat16),
        conv_grad,
    )


def solution(mesh):
    placed = (
        P("tm", "head"),
        P("tm", "head"),
        P("tm", "head"),
        P("tm", "head"),
        P("head"),
        P(None, "head"),
        P("tm", None),
        P("tm", None),
    )
    return jax.shard_map(
        body,
        mesh=mesh,
        in_specs=placed,
        out_specs=(P("tm", "head"), P("tm", "head"), P("tm", "head"), P(None, "head")),
        check_vma=False,
    )
```

```python
import jax
import jax.numpy as jnp
from jax import lax
from jax.sharding import PartitionSpec as P

D = 2048
HD = 128
BLK = 128
REACH = 3
WIN = 6


NEG_FILL = -1e30
NORM_EPS = 1e-06


def from_behind(block, axis, distance):
    devices = range(lax.axis_size(axis))
    route = [(i - distance, i) for i in devices if i - distance in devices]
    return lax.ppermute(block, axis, route)


def chip_swap(block, axis):
    size = lax.axis_size(axis)
    return lax.ppermute(block, axis, [(i, i ^ 1) for i in range(size)])


def all_sum(block, axis):
    size = lax.axis_size(axis)
    if size & (size - 1):
        return lax.psum(block, axis)
    stride = 1
    while stride < size:
        block = block + lax.ppermute(block, axis, [(i, i ^ stride) for i in range(size)])
        stride *= 2
    return block


def pair_sum(block, axis):
    if lax.axis_size(axis) != 2:
        return lax.psum(block, axis)
    return block + lax.ppermute(block, axis, [(0, 1), (1, 0)])


def split_heads(array):
    return array.reshape(array.shape[0], array.shape[1] // HD, HD)


def window_mask(block_bits, device, row_count, key_count):
    per_device = row_count // BLK
    key_blocks = key_count // BLK
    first_block = device * per_device - (key_blocks - per_device)
    qb = jnp.arange(per_device, dtype=jnp.int32)
    kb = jnp.arange(key_blocks, dtype=jnp.int32)
    relative = qb[:, None] + (key_blocks - per_device) - kb[None, :]
    one_hot = relative[:, :, None] == jnp.arange(WIN, dtype=jnp.int32)[None, None, :]
    picked_bits = jnp.sum(jnp.where(one_hot, block_bits[:, None, :], 0), axis=2)
    coarse = (picked_bits > 0) & (relative >= 0) & (relative < WIN) & (first_block + kb[None, :] >= 0)
    fine = jnp.repeat(jnp.repeat(coarse, BLK, axis=0), BLK, axis=1)
    q = jnp.arange(row_count, dtype=jnp.int32)
    s = jnp.arange(key_count, dtype=jnp.int32)
    causal = s[None, :] <= q[:, None] + (key_count - row_count)
    return fine & causal


def body(queries, keys, values_in, teacher, gain, conv_weight, block_bits, mask_pos):
    row_count, channels = queries.shape
    tap_count = conv_weight.shape[0]
    rim_rows = tap_count - 1
    device = lax.axis_index("tm")
    even = device % 2 == 0
    score_scale = HD ** (-0.5)
    far_rows = row_count - BLK
    far_lead = 8
    key_count = REACH * row_count + (row_count - far_rows)

    def relay(own, second):
        first = chip_swap(jnp.where(even, own, second), "tm")
        third = from_behind(second[far_rows - far_lead :], "tm", 1)
        return jnp.concatenate([third, second, first, own], 0)

    key_second = from_behind(keys, "tm", 2)
    key_second, values_in = lax.optimization_barrier((key_second, values_in))
    key_win = relay(keys, key_second)[far_lead:]
    value_second = from_behind(values_in, "tm", 2)

    heads_query = split_heads(queries)
    heads_key = split_heads(key_win)
    mask = window_mask(block_bits, device, row_count, key_count)

    raw_scores = (
        jnp.einsum("thd,uhd->htu", heads_query, heads_key, preferred_element_type=jnp.float32)
        * score_scale
    )
    scores = jnp.where(mask[None], raw_scores, NEG_FILL)
    row_peak = jnp.max(scores, axis=2)
    expo = jnp.where(mask[None], jnp.exp(scores - row_peak[..., None]), 0.0)
    row_total = jnp.sum(expo, axis=2)
    value_second, row_total = lax.optimization_barrier((value_second, row_total))
    vin_win = relay(values_in, value_second)
    conv_sum = jnp.zeros((key_count, channels), jnp.float32)
    for tap_index in range(tap_count):
        conv_sum = conv_sum + conv_weight[tap_index] * vin_win[
            far_lead - tap_index : far_lead - tap_index + key_count
        ].astype(jnp.float32)
    value_win = conv_sum.astype(jnp.bfloat16)
    heads_value = split_heads(value_win)
    prob = expo / row_total[..., None]
    weights = prob.astype(jnp.bfloat16)
    attended = jnp.einsum("htu,uhd->thd", weights, heads_value, preferred_element_type=jnp.float32)

    flattened = attended.reshape(row_count, channels)
    position = jnp.arange(row_count, dtype=jnp.int32) % BLK
    chosen = jnp.any(jnp.repeat(mask_pos, BLK, axis=0) == position[:, None], axis=1)
    weighted = flattened * gain
    sums = pair_sum(
        jnp.stack(
            [
                jnp.sum(flattened * flattened, axis=1),
                jnp.sum(weighted * weighted, axis=1),
                jnp.sum(teacher.astype(jnp.float32) * weighted, axis=1),
            ]
        ),
        "head",
    )
    squares = sums[0]
    inverse = lax.rsqrt(squares / D + NORM_EPS)
    prediction = flattened * inverse[:, None] * gain
    residual = jnp.where(chosen[:, None], prediction - teacher.astype(jnp.float32), 0.0)
    scaled = residual * gain
    cross_term = jnp.where(chosen, inverse * sums[1] - sums[2], 0.0)
    out_grad = (
        inverse[:, None] * scaled - flattened * (inverse**3 * cross_term / D)[:, None]
    ).astype(jnp.bfloat16)
    heads_grad = split_heads(out_grad)
    delta = jnp.sum(heads_grad.astype(jnp.float32) * attended, axis=2).T

    prob_grad = jnp.einsum("thd,uhd->htu", heads_grad, heads_value, preferred_element_type=jnp.float32)
    score_grad = (prob * (prob_grad - delta[:, :, None])).astype(jnp.bfloat16)
    query_grad = (
        jnp.einsum("htu,uhd->thd", score_grad, heads_key, preferred_element_type=jnp.float32)
        * score_scale
    )
    key_part = (
        jnp.einsum("htu,thd->uhd", score_grad, heads_query, preferred_element_type=jnp.float32)
        * score_scale
    ).reshape(key_count, channels)
    value_part = jnp.einsum(
        "htu,thd->uhd", weights, heads_grad, preferred_element_type=jnp.float32
    ).reshape(key_count, channels)

    local_taps = jnp.stack(
        [
            jnp.sum(
                value_part
                * vin_win[far_lead - tap_index : far_lead - tap_index + key_count].astype(jnp.float32),
                axis=0,
            )
            for tap_index in range(tap_count)
        ]
    )
    conv_grad = all_sum(local_taps, "tm")

    lead = jnp.zeros((far_lead, channels), jnp.float32)
    padded_value = jnp.concatenate([lead, value_part, jnp.zeros((rim_rows, channels), jnp.float32)], 0)
    value_sum = jnp.zeros((key_count + far_lead, channels), jnp.float32)
    for tap_index in range(tap_count):
        value_sum = value_sum + conv_weight[tap_index] * padded_value[tap_index : tap_index + key_count + far_lead]

    def relay_back(grads):
        cut_third = row_count - far_rows + far_lead
        grad_third = grads[:cut_third]
        grad_second = grads[cut_third : cut_third + row_count]
        grad_first = grads[cut_third + row_count : cut_third + 2 * row_count]
        grad_own = grads[cut_third + 2 * row_count :]
        back_third = from_behind(grad_third.astype(jnp.bfloat16), "tm", -1).astype(jnp.float32)
        back_first = chip_swap(grad_first.astype(jnp.bfloat16), "tm").astype(jnp.float32)
        grad_second = grad_second + jnp.concatenate(
            [jnp.zeros((far_rows - far_lead, grads.shape[1]), jnp.float32), back_third], 0
        )
        grad_second = grad_second + jnp.where(even, 0.0, back_first)
        back_second = from_behind(grad_second.astype(jnp.bfloat16), "tm", -2).astype(jnp.float32)
        return grad_own + jnp.where(even, back_first, 0.0) + back_second

    value_total = relay_back(value_sum)
    key_total = relay_back(jnp.concatenate([lead, key_part], 0))

    return (
        query_grad.reshape(row_count, channels).astype(jnp.bfloat16),
        key_total.astype(jnp.bfloat16),
        value_total.astype(jnp.bfloat16),
        conv_grad,
    )


def solution(mesh):
    placed = (
        P("tm", "head"),
        P("tm", "head"),
        P("tm", "head"),
        P("tm", "head"),
        P("head"),
        P(None, "head"),
        P("tm", None),
        P("tm", None),
    )
    return jax.shard_map(
        body,
        mesh=mesh,
        in_specs=placed,
        out_specs=(P("tm", "head"), P("tm", "head"), P("tm", "head"), P(None, "head")),
        check_vma=False,
    )
```

```python
import jax
import jax.numpy as jnp
from jax import lax
from jax.sharding import PartitionSpec as P

D = 2048
HD = 128
BLK = 128
REACH = 3
WIN = 6


NEG_FILL = -1e30
NORM_EPS = 1e-06


def from_behind(block, axis, distance):
    devices = range(lax.axis_size(axis))
    route = [(i - distance, i) for i in devices if i - distance in devices]
    return lax.ppermute(block, axis, route)


def chip_swap(block, axis):
    size = lax.axis_size(axis)
    return lax.ppermute(block, axis, [(i, i ^ 1) for i in range(size)])


def exchange_rounds(block, axis, first, last):
    size = lax.axis_size(axis)
    stride = first
    while stride < min(last, size):
        block = block + lax.ppermute(block, axis, [(i, i ^ stride) for i in range(size)])
        stride *= 2
    return block


def pair_sum(block, axis):
    if lax.axis_size(axis) != 2:
        return lax.psum(block, axis)
    return block + lax.ppermute(block, axis, [(0, 1), (1, 0)])


def split_heads(array):
    return array.reshape(array.shape[0], array.shape[1] // HD, HD)


def window_mask(block_bits, device, row_count, key_count):
    per_device = row_count // BLK
    key_blocks = key_count // BLK
    first_block = device * per_device - (key_blocks - per_device)
    qb = jnp.arange(per_device, dtype=jnp.int32)
    kb = jnp.arange(key_blocks, dtype=jnp.int32)
    relative = qb[:, None] + (key_blocks - per_device) - kb[None, :]
    one_hot = relative[:, :, None] == jnp.arange(WIN, dtype=jnp.int32)[None, None, :]
    picked_bits = jnp.sum(jnp.where(one_hot, block_bits[:, None, :], 0), axis=2)
    coarse = (picked_bits > 0) & (relative >= 0) & (relative < WIN) & (first_block + kb[None, :] >= 0)
    fine = jnp.repeat(jnp.repeat(coarse, BLK, axis=0), BLK, axis=1)
    q = jnp.arange(row_count, dtype=jnp.int32)
    s = jnp.arange(key_count, dtype=jnp.int32)
    causal = s[None, :] <= q[:, None] + (key_count - row_count)
    return fine & causal


def body(queries, keys, values_in, teacher, gain, conv_weight, block_bits, mask_pos):
    row_count, channels = queries.shape
    tap_count = conv_weight.shape[0]
    rim_rows = tap_count - 1
    device = lax.axis_index("tm")
    even = device % 2 == 0
    score_scale = HD ** (-0.5)
    far_rows = row_count - BLK
    far_lead = 8
    key_count = REACH * row_count + (row_count - far_rows)

    def relay(own):
        second = from_behind(own, "tm", 2)
        first = chip_swap(jnp.where(even, own, second), "tm")
        third = from_behind(second[far_rows - far_lead :], "tm", 1)
        return jnp.concatenate([third, second, first, own], 0)

    key_win = relay(keys)[far_lead:]
    vin_win = relay(values_in)

    conv_sum = jnp.zeros((key_count, channels), jnp.float32)
    for tap_index in range(tap_count):
        conv_sum = conv_sum + conv_weight[tap_index] * vin_win[
            far_lead - tap_index : far_lead - tap_index + key_count
        ].astype(jnp.float32)
    value_win = conv_sum.astype(jnp.bfloat16)

    heads_query = split_heads(queries)
    heads_key = split_heads(key_win)
    heads_value = split_heads(value_win)
    mask = window_mask(block_bits, device, row_count, key_count)

    raw_scores = (
        jnp.einsum("thd,uhd->htu", heads_query, heads_key, preferred_element_type=jnp.float32)
        * score_scale
    )
    scores = jnp.where(mask[None], raw_scores, NEG_FILL)
    row_peak = jnp.max(scores, axis=2)
    expo = jnp.where(mask[None], jnp.exp(scores - row_peak[..., None]), 0.0)
    row_total = jnp.sum(expo, axis=2)
    prob = expo / row_total[..., None]
    weights = prob.astype(jnp.bfloat16)
    attended = jnp.einsum("htu,uhd->thd", weights, heads_value, preferred_element_type=jnp.float32)

    flattened = attended.reshape(row_count, channels)
    position = jnp.arange(row_count, dtype=jnp.int32) % BLK
    chosen = jnp.any(jnp.repeat(mask_pos, BLK, axis=0) == position[:, None], axis=1)
    weighted = flattened * gain
    sums = pair_sum(
        jnp.stack(
            [
                jnp.sum(flattened * flattened, axis=1),
                jnp.sum(weighted * weighted, axis=1),
                jnp.sum(teacher.astype(jnp.float32) * weighted, axis=1),
            ]
        ),
        "head",
    )
    squares = sums[0]
    inverse = lax.rsqrt(squares / D + NORM_EPS)
    prediction = flattened * inverse[:, None] * gain
    residual = jnp.where(chosen[:, None], prediction - teacher.astype(jnp.float32), 0.0)
    scaled = residual * gain
    cross_term = jnp.where(chosen, inverse * sums[1] - sums[2], 0.0)
    out_grad = (
        inverse[:, None] * scaled - flattened * (inverse**3 * cross_term / D)[:, None]
    ).astype(jnp.bfloat16)
    heads_grad = split_heads(out_grad)
    delta = jnp.sum(heads_grad.astype(jnp.float32) * attended, axis=2).T

    prob_grad = jnp.einsum("thd,uhd->htu", heads_grad, heads_value, preferred_element_type=jnp.float32)
    score_grad = (prob * (prob_grad - delta[:, :, None])).astype(jnp.bfloat16)
    query_grad = (
        jnp.einsum("htu,uhd->thd", score_grad, heads_key, preferred_element_type=jnp.float32)
        * score_scale
    )
    key_part = (
        jnp.einsum("htu,thd->uhd", score_grad, heads_query, preferred_element_type=jnp.float32)
        * score_scale
    ).reshape(key_count, channels)
    value_part = jnp.einsum(
        "htu,thd->uhd", weights, heads_grad, preferred_element_type=jnp.float32
    ).reshape(key_count, channels)

    local_taps = jnp.stack(
        [
            jnp.sum(
                value_part
                * vin_win[far_lead - tap_index : far_lead - tap_index + key_count].astype(jnp.float32),
                axis=0,
            )
            for tap_index in range(tap_count)
        ]
    )

    lead = jnp.zeros((far_lead, channels), jnp.float32)
    padded_value = jnp.concatenate([lead, value_part, jnp.zeros((rim_rows, channels), jnp.float32)], 0)
    value_sum = jnp.zeros((key_count + far_lead, channels), jnp.float32)
    for tap_index in range(tap_count):
        value_sum = value_sum + conv_weight[tap_index] * padded_value[tap_index : tap_index + key_count + far_lead]

    def relay_back_first(grads):
        cut_third = row_count - far_rows + far_lead
        grad_third = grads[:cut_third]
        grad_second = grads[cut_third : cut_third + row_count]
        grad_first = grads[cut_third + row_count : cut_third + 2 * row_count]
        grad_own = grads[cut_third + 2 * row_count :]
        back_third = from_behind(grad_third.astype(jnp.bfloat16), "tm", -1).astype(jnp.float32)
        back_first = chip_swap(grad_first.astype(jnp.bfloat16), "tm").astype(jnp.float32)
        grad_second = grad_second + jnp.concatenate(
            [jnp.zeros((far_rows - far_lead, grads.shape[1]), jnp.float32), back_third], 0
        )
        grad_second = grad_second + jnp.where(even, 0.0, back_first)
        return grad_own + jnp.where(even, back_first, 0.0), grad_second.astype(jnp.bfloat16)

    value_near, value_second = relay_back_first(value_sum)
    key_near, key_second = relay_back_first(jnp.concatenate([lead, key_part], 0))

    size = lax.axis_size("tm")
    if size & (size - 1):
        conv_grad = lax.psum(local_taps, "tm")
    else:
        split = max(1, size // 4)
        taps_near = exchange_rounds(local_taps, "tm", 1, split)
        taps_near, value_second, key_second = lax.optimization_barrier((taps_near, value_second, key_second))
        conv_grad = exchange_rounds(taps_near, "tm", split, size)
    value_total = value_near + from_behind(value_second, "tm", -2).astype(jnp.float32)
    key_total = key_near + from_behind(key_second, "tm", -2).astype(jnp.float32)

    return (
        query_grad.reshape(row_count, channels).astype(jnp.bfloat16),
        key_total.astype(jnp.bfloat16),
        value_total.astype(jnp.bfloat16),
        conv_grad,
    )


def solution(mesh):
    placed = (
        P("tm", "head"),
        P("tm", "head"),
        P("tm", "head"),
        P("tm", "head"),
        P("head"),
        P(None, "head"),
        P("tm", None),
        P("tm", None),
    )
    return jax.shard_map(
        body,
        mesh=mesh,
        in_specs=placed,
        out_specs=(P("tm", "head"), P("tm", "head"), P("tm", "head"), P(None, "head")),
        check_vma=False,
    )
```

```python
import jax
import jax.numpy as jnp
from jax import lax
from jax.sharding import PartitionSpec as P

D = 2048
HD = 128
BLK = 128
REACH = 3
WIN = 6


NEG_FILL = -1e30
NORM_EPS = 1e-06


def from_behind(block, axis, distance):
    devices = range(lax.axis_size(axis))
    route = [(i - distance, i) for i in devices if i - distance in devices]
    return lax.ppermute(block, axis, route)


def chip_swap(block, axis):
    size = lax.axis_size(axis)
    return lax.ppermute(block, axis, [(i, i ^ 1) for i in range(size)])


def all_sum(block, axis):
    size = lax.axis_size(axis)
    if size & (size - 1):
        return lax.psum(block, axis)
    stride = 1
    while stride < size:
        block = block + lax.ppermute(block, axis, [(i, i ^ stride) for i in range(size)])
        stride *= 2
    return block


def pair_sum(block, axis):
    if lax.axis_size(axis) != 2:
        return lax.psum(block, axis)
    return block + lax.ppermute(block, axis, [(0, 1), (1, 0)])


def split_heads(array):
    return array.reshape(array.shape[0], array.shape[1] // HD, HD)


def window_mask(block_bits, device, row_count, key_count):
    per_device = row_count // BLK
    key_blocks = key_count // BLK
    first_block = device * per_device - (key_blocks - per_device)
    qb = jnp.arange(per_device, dtype=jnp.int32)
    kb = jnp.arange(key_blocks, dtype=jnp.int32)
    relative = qb[:, None] + (key_blocks - per_device) - kb[None, :]
    one_hot = relative[:, :, None] == jnp.arange(WIN, dtype=jnp.int32)[None, None, :]
    picked_bits = jnp.sum(jnp.where(one_hot, block_bits[:, None, :], 0), axis=2)
    coarse = (picked_bits > 0) & (relative >= 0) & (relative < WIN) & (first_block + kb[None, :] >= 0)
    fine = jnp.repeat(jnp.repeat(coarse, BLK, axis=0), BLK, axis=1)
    q = jnp.arange(row_count, dtype=jnp.int32)
    s = jnp.arange(key_count, dtype=jnp.int32)
    causal = s[None, :] <= q[:, None] + (key_count - row_count)
    return fine & causal


def body(queries, keys, values_in, teacher, gain, conv_weight, block_bits, mask_pos):
    row_count, channels = queries.shape
    tap_count = conv_weight.shape[0]
    rim_rows = tap_count - 1
    device = lax.axis_index("tm")
    even = device % 2 == 0
    score_scale = HD ** (-0.5)
    far_rows = row_count - BLK
    far_lead = 8
    key_count = REACH * row_count + (row_count - far_rows)

    def relay(own):
        second = from_behind(own, "tm", 2)
        first = chip_swap(jnp.where(even, own, second), "tm")
        third = from_behind(second[far_rows - far_lead :], "tm", 1)
        return jnp.concatenate([third, second, first, own], 0)

    key_win = relay(keys)[far_lead:]
    vin_win = relay(values_in)

    conv_sum = jnp.zeros((key_count, channels), jnp.float32)
    for tap_index in range(tap_count):
        conv_sum = conv_sum + conv_weight[tap_index] * vin_win[
            far_lead - tap_index : far_lead - tap_index + key_count
        ].astype(jnp.float32)
    value_win = conv_sum.astype(jnp.bfloat16)

    heads_query = split_heads(queries)
    heads_key = split_heads(key_win)
    heads_value = split_heads(value_win)
    mask = window_mask(block_bits, device, row_count, key_count)

    raw_scores = (
        jnp.einsum("thd,uhd->htu", heads_query, heads_key, preferred_element_type=jnp.float32)
        * score_scale
    )
    scores = jnp.where(mask[None], raw_scores, NEG_FILL)
    row_peak = jnp.max(scores, axis=2)
    expo = jnp.where(mask[None], jnp.exp(scores - row_peak[..., None]), 0.0)
    row_total = jnp.sum(expo, axis=2)
    prob = expo / row_total[..., None]
    weights = prob.astype(jnp.bfloat16)
    attended = jnp.einsum("htu,uhd->thd", weights, heads_value, preferred_element_type=jnp.float32)

    flattened = attended.reshape(row_count, channels)
    position = jnp.arange(row_count, dtype=jnp.int32) % BLK
    chosen = jnp.any(jnp.repeat(mask_pos, BLK, axis=0) == position[:, None], axis=1)
    weighted = flattened * gain
    sums = pair_sum(
        jnp.stack(
            [
                jnp.sum(flattened * flattened, axis=1),
                jnp.sum(weighted * weighted, axis=1),
                jnp.sum(teacher.astype(jnp.float32) * weighted, axis=1),
            ]
        ),
        "head",
    )
    squares = sums[0]
    inverse = lax.rsqrt(squares / D + NORM_EPS)
    prediction = flattened * inverse[:, None] * gain
    residual = jnp.where(chosen[:, None], prediction - teacher.astype(jnp.float32), 0.0)
    scaled = residual * gain
    cross_term = jnp.where(chosen, inverse * sums[1] - sums[2], 0.0)
    out_grad = (
        inverse[:, None] * scaled - flattened * (inverse**3 * cross_term / D)[:, None]
    ).astype(jnp.bfloat16)
    heads_grad = split_heads(out_grad)
    delta = jnp.sum(heads_grad.astype(jnp.float32) * attended, axis=2).T

    prob_grad = jnp.einsum("thd,uhd->htu", heads_grad, heads_value, preferred_element_type=jnp.float32)
    score_grad = (prob * (prob_grad - delta[:, :, None])).astype(jnp.bfloat16)
    query_grad = (
        jnp.einsum("htu,uhd->thd", score_grad, heads_key, preferred_element_type=jnp.float32)
        * score_scale
    )
    key_part = (
        jnp.einsum("htu,thd->uhd", score_grad, heads_query, preferred_element_type=jnp.float32)
        * score_scale
    ).reshape(key_count, channels)
    value_part = jnp.einsum(
        "htu,thd->uhd", weights, heads_grad, preferred_element_type=jnp.float32
    ).reshape(key_count, channels)

    local_taps = jnp.stack(
        [
            jnp.sum(
                value_part
                * vin_win[far_lead - tap_index : far_lead - tap_index + key_count].astype(jnp.float32),
                axis=0,
            )
            for tap_index in range(tap_count)
        ]
    )
    conv_grad = all_sum(local_taps, "tm")

    lead = jnp.zeros((far_lead, channels), jnp.float32)

    def relay_back_first(grads):
        cut_third = row_count - far_rows + far_lead
        grad_third = grads[:cut_third]
        grad_second = grads[cut_third : cut_third + row_count]
        grad_first = grads[cut_third + row_count : cut_third + 2 * row_count]
        grad_own = grads[cut_third + 2 * row_count :]
        back_third = from_behind(grad_third.astype(jnp.bfloat16), "tm", -1).astype(jnp.float32)
        back_first = chip_swap(grad_first.astype(jnp.bfloat16), "tm").astype(jnp.float32)
        grad_second = grad_second + jnp.concatenate(
            [jnp.zeros((far_rows - far_lead, grads.shape[1]), jnp.float32), back_third], 0
        )
        grad_second = grad_second + jnp.where(even, 0.0, back_first)
        return grad_own + jnp.where(even, back_first, 0.0), grad_second.astype(jnp.bfloat16)

    def relay_back(grads):
        near, second = relay_back_first(grads)
        return near + from_behind(second, "tm", -2).astype(jnp.float32)

    key_near, key_second = relay_back_first(jnp.concatenate([lead, key_part], 0))
    key_near, key_second, value_part = lax.optimization_barrier((key_near, key_second, value_part))
    key_total = key_near + from_behind(key_second, "tm", -2).astype(jnp.float32)

    padded_value = jnp.concatenate([lead, value_part, jnp.zeros((rim_rows, channels), jnp.float32)], 0)
    value_sum = jnp.zeros((key_count + far_lead, channels), jnp.float32)
    for tap_index in range(tap_count):
        value_sum = value_sum + conv_weight[tap_index] * padded_value[tap_index : tap_index + key_count + far_lead]
    value_total = relay_back(value_sum)

    return (
        query_grad.reshape(row_count, channels).astype(jnp.bfloat16),
        key_total.astype(jnp.bfloat16),
        value_total.astype(jnp.bfloat16),
        conv_grad,
    )


def solution(mesh):
    placed = (
        P("tm", "head"),
        P("tm", "head"),
        P("tm", "head"),
        P("tm", "head"),
        P("head"),
        P(None, "head"),
        P("tm", None),
        P("tm", None),
    )
    return jax.shard_map(
        body,
        mesh=mesh,
        in_specs=placed,
        out_specs=(P("tm", "head"), P("tm", "head"), P("tm", "head"), P(None, "head")),
        check_vma=False,
    )
```

```python
import jax
import jax.numpy as jnp
from jax import lax
from jax.sharding import PartitionSpec as P

D = 2048
HD = 128
BLK = 128
REACH = 3
WIN = 6


NEG_FILL = -1e30
NORM_EPS = 1e-06


def from_behind(block, axis, distance):
    devices = range(lax.axis_size(axis))
    route = [(i - distance, i) for i in devices if i - distance in devices]
    return lax.ppermute(block, axis, route)


def chip_swap(block, axis):
    size = lax.axis_size(axis)
    return lax.ppermute(block, axis, [(i, i ^ 1) for i in range(size)])


def all_sum(block, axis):
    size = lax.axis_size(axis)
    if size & (size - 1):
        return lax.psum(block, axis)
    stride = 1
    while stride < size:
        block = block + lax.ppermute(block, axis, [(i, i ^ stride) for i in range(size)])
        stride *= 2
    return block


def pair_sum(block, axis):
    if lax.axis_size(axis) != 2:
        return lax.psum(block, axis)
    return block + lax.ppermute(block, axis, [(0, 1), (1, 0)])


def split_heads(array):
    return array.reshape(array.shape[0], array.shape[1] // HD, HD)


def window_mask(block_bits, device, row_count, key_count):
    per_device = row_count // BLK
    key_blocks = key_count // BLK
    first_block = device * per_device - (key_blocks - per_device)
    qb = jnp.arange(per_device, dtype=jnp.int32)
    kb = jnp.arange(key_blocks, dtype=jnp.int32)
    relative = qb[:, None] + (key_blocks - per_device) - kb[None, :]
    one_hot = relative[:, :, None] == jnp.arange(WIN, dtype=jnp.int32)[None, None, :]
    picked_bits = jnp.sum(jnp.where(one_hot, block_bits[:, None, :], 0), axis=2)
    coarse = (picked_bits > 0) & (relative >= 0) & (relative < WIN) & (first_block + kb[None, :] >= 0)
    fine = jnp.repeat(jnp.repeat(coarse, BLK, axis=0), BLK, axis=1)
    q = jnp.arange(row_count, dtype=jnp.int32)
    s = jnp.arange(key_count, dtype=jnp.int32)
    causal = s[None, :] <= q[:, None] + (key_count - row_count)
    return fine & causal


def body(queries, keys, values_in, teacher, gain, conv_weight, block_bits, mask_pos):
    row_count, channels = queries.shape
    tap_count = conv_weight.shape[0]
    rim_rows = tap_count - 1
    device = lax.axis_index("tm")
    even = device % 2 == 0
    score_scale = HD ** (-0.5)
    far_rows = row_count - BLK
    far_lead = 8
    key_count = REACH * row_count + (row_count - far_rows)

    def relay(own):
        second = from_behind(own, "tm", 2)
        first = chip_swap(jnp.where(even, own, second), "tm")
        third = from_behind(second[far_rows - far_lead :], "tm", 1)
        return jnp.concatenate([third, second, first, own], 0)

    key_win = relay(keys)[far_lead:]
    vin_win = relay(values_in)

    conv_sum = jnp.zeros((key_count, channels), jnp.float32)
    for tap_index in range(tap_count):
        conv_sum = conv_sum + conv_weight[tap_index] * vin_win[
            far_lead - tap_index : far_lead - tap_index + key_count
        ].astype(jnp.float32)
    value_win = conv_sum.astype(jnp.bfloat16)

    heads_query = split_heads(queries)
    heads_key = split_heads(key_win)
    heads_value = split_heads(value_win)
    mask = window_mask(block_bits, device, row_count, key_count)

    raw_scores = (
        jnp.einsum("thd,uhd->htu", heads_query, heads_key, preferred_element_type=jnp.float32)
        * score_scale
    )
    scores = jnp.where(mask[None], raw_scores, NEG_FILL)
    row_peak = jnp.max(scores, axis=2)
    expo = jnp.where(mask[None], jnp.exp(scores - row_peak[..., None]), 0.0)
    row_total = jnp.sum(expo, axis=2)
    prob = expo / row_total[..., None]
    weights = prob.astype(jnp.bfloat16)
    attended = jnp.einsum("htu,uhd->thd", weights, heads_value, preferred_element_type=jnp.float32)

    flattened = attended.reshape(row_count, channels)
    position = jnp.arange(row_count, dtype=jnp.int32) % BLK
    chosen = jnp.any(jnp.repeat(mask_pos, BLK, axis=0) == position[:, None], axis=1)
    weighted = flattened * gain
    sums = pair_sum(
        jnp.stack(
            [
                jnp.sum(flattened * flattened, axis=1),
                jnp.sum(weighted * weighted, axis=1),
                jnp.sum(teacher.astype(jnp.float32) * weighted, axis=1),
            ]
        ),
        "head",
    )
    squares = sums[0]
    inverse = lax.rsqrt(squares / D + NORM_EPS)
    prediction = flattened * inverse[:, None] * gain
    residual = jnp.where(chosen[:, None], prediction - teacher.astype(jnp.float32), 0.0)
    scaled = residual * gain
    cross_term = jnp.where(chosen, inverse * sums[1] - sums[2], 0.0)
    out_grad = (
        inverse[:, None] * scaled - flattened * (inverse**3 * cross_term / D)[:, None]
    ).astype(jnp.bfloat16)
    heads_grad = split_heads(out_grad)
    delta = jnp.sum(heads_grad.astype(jnp.float32) * attended, axis=2).T

    prob_grad = jnp.einsum("thd,uhd->htu", heads_grad, heads_value, preferred_element_type=jnp.float32)
    score_grad = (prob * (prob_grad - delta[:, :, None])).astype(jnp.bfloat16)
    query_grad = (
        jnp.einsum("htu,uhd->thd", score_grad, heads_key, preferred_element_type=jnp.float32)
        * score_scale
    )
    key_part = (
        jnp.einsum("htu,thd->uhd", score_grad, heads_query, preferred_element_type=jnp.float32)
        * score_scale
    ).reshape(key_count, channels)
    value_part = jnp.einsum(
        "htu,thd->uhd", weights, heads_grad, preferred_element_type=jnp.float32
    ).reshape(key_count, channels)

    local_taps = jnp.stack(
        [
            jnp.sum(
                value_part
                * vin_win[far_lead - tap_index : far_lead - tap_index + key_count].astype(jnp.float32),
                axis=0,
            )
            for tap_index in range(tap_count)
        ]
    )
    conv_grad = all_sum(local_taps, "tm")

    lead = jnp.zeros((far_lead, channels), jnp.float32)
    padded_value = jnp.concatenate([lead, value_part, jnp.zeros((rim_rows, channels), jnp.float32)], 0)
    value_sum = jnp.zeros((key_count + far_lead, channels), jnp.float32)
    for tap_index in range(tap_count):
        value_sum = value_sum + conv_weight[tap_index] * padded_value[tap_index : tap_index + key_count + far_lead]

    def parts(grads):
        cut_third = row_count - far_rows + far_lead
        return (
            grads[:cut_third],
            grads[cut_third : cut_third + row_count],
            grads[cut_third + row_count : cut_third + 2 * row_count],
            grads[cut_third + 2 * row_count :],
        )

    key_grads = jnp.concatenate([lead, key_part], 0)
    value_third, value_second, value_first, value_own = parts(value_sum)
    key_third, key_second, key_first, key_own = parts(key_grads)
    value_back_first = chip_swap(value_first.astype(jnp.bfloat16), "tm").astype(jnp.float32)
    key_back_first = chip_swap(key_first.astype(jnp.bfloat16), "tm").astype(jnp.float32)
    back_third = from_behind(
        jnp.concatenate([value_third, key_third], 1).astype(jnp.bfloat16), "tm", -1
    ).astype(jnp.float32)
    spacer = jnp.zeros((far_rows - far_lead, 2 * channels), jnp.float32)
    both_second = jnp.concatenate([value_second, key_second], 1) + jnp.concatenate([spacer, back_third], 0)
    both_first = jnp.concatenate([value_back_first, key_back_first], 1)
    both_second = both_second + jnp.where(even, 0.0, both_first)
    back_second = from_behind(both_second.astype(jnp.bfloat16), "tm", -2).astype(jnp.float32)
    both_total = (
        jnp.concatenate([value_own, key_own], 1) + jnp.where(even, both_first, 0.0) + back_second
    )
    value_total = both_total[:, :channels]
    key_total = both_total[:, channels:]

    return (
        query_grad.reshape(row_count, channels).astype(jnp.bfloat16),
        key_total.astype(jnp.bfloat16),
        value_total.astype(jnp.bfloat16),
        conv_grad,
    )


def solution(mesh):
    placed = (
        P("tm", "head"),
        P("tm", "head"),
        P("tm", "head"),
        P("tm", "head"),
        P("head"),
        P(None, "head"),
        P("tm", None),
        P("tm", None),
    )
    return jax.shard_map(
        body,
        mesh=mesh,
        in_specs=placed,
        out_specs=(P("tm", "head"), P("tm", "head"), P("tm", "head"), P(None, "head")),
        check_vma=False,
    )
```

```python
import jax
import jax.numpy as jnp
from jax import lax
from jax.sharding import PartitionSpec as P

D = 2048
HD = 128
BLK = 128
REACH = 3
WIN = 6


NEG_FILL = -1e30
NORM_EPS = 1e-06


def from_behind(block, axis, distance):
    devices = range(lax.axis_size(axis))
    route = [(i - distance, i) for i in devices if i - distance in devices]
    return lax.ppermute(block, axis, route)


def chip_swap(block, axis):
    size = lax.axis_size(axis)
    return lax.ppermute(block, axis, [(i, i ^ 1) for i in range(size)])


def all_sum(block, axis, radix=4):
    size = lax.axis_size(axis)
    if size & (size - 1):
        return lax.psum(block, axis)
    index = lax.axis_index(axis)
    stride = 1
    while stride < size:
        group = min(radix, size // stride)
        digit = (index // stride) % group
        received = [block]
        for step in range(1, group):
            route = []
            for i in range(size):
                own = (i // stride) % group
                route.append((i, i + ((own + step) % group - own) * stride))
            received.append(lax.ppermute(block, axis, route))
        stacked = jnp.stack(received)
        total = None
        for source in range(group):
            term = lax.dynamic_index_in_dim(stacked, (digit - source) % group, 0, keepdims=False)
            total = term if total is None else total + term
        block = total
        stride *= group
    return block


def pair_sum(block, axis):
    if lax.axis_size(axis) != 2:
        return lax.psum(block, axis)
    return block + lax.ppermute(block, axis, [(0, 1), (1, 0)])


def split_heads(array):
    return array.reshape(array.shape[0], array.shape[1] // HD, HD)


def window_mask(block_bits, device, row_count, key_count):
    per_device = row_count // BLK
    key_blocks = key_count // BLK
    first_block = device * per_device - (key_blocks - per_device)
    qb = jnp.arange(per_device, dtype=jnp.int32)
    kb = jnp.arange(key_blocks, dtype=jnp.int32)
    relative = qb[:, None] + (key_blocks - per_device) - kb[None, :]
    one_hot = relative[:, :, None] == jnp.arange(WIN, dtype=jnp.int32)[None, None, :]
    picked_bits = jnp.sum(jnp.where(one_hot, block_bits[:, None, :], 0), axis=2)
    coarse = (picked_bits > 0) & (relative >= 0) & (relative < WIN) & (first_block + kb[None, :] >= 0)
    fine = jnp.repeat(jnp.repeat(coarse, BLK, axis=0), BLK, axis=1)
    q = jnp.arange(row_count, dtype=jnp.int32)
    s = jnp.arange(key_count, dtype=jnp.int32)
    causal = s[None, :] <= q[:, None] + (key_count - row_count)
    return fine & causal


def body(queries, keys, values_in, teacher, gain, conv_weight, block_bits, mask_pos):
    row_count, channels = queries.shape
    tap_count = conv_weight.shape[0]
    rim_rows = tap_count - 1
    device = lax.axis_index("tm")
    even = device % 2 == 0
    score_scale = HD ** (-0.5)
    far_rows = row_count - BLK
    far_lead = 8
    key_count = REACH * row_count + (row_count - far_rows)

    def relay(own):
        second = from_behind(own, "tm", 2)
        first = chip_swap(jnp.where(even, own, second), "tm")
        third = from_behind(second[far_rows - far_lead :], "tm", 1)
        return jnp.concatenate([third, second, first, own], 0)

    key_win = relay(keys)[far_lead:]
    vin_win = relay(values_in)

    conv_sum = jnp.zeros((key_count, channels), jnp.float32)
    for tap_index in range(tap_count):
        conv_sum = conv_sum + conv_weight[tap_index] * vin_win[
            far_lead - tap_index : far_lead - tap_index + key_count
        ].astype(jnp.float32)
    value_win = conv_sum.astype(jnp.bfloat16)

    heads_query = split_heads(queries)
    heads_key = split_heads(key_win)
    heads_value = split_heads(value_win)
    mask = window_mask(block_bits, device, row_count, key_count)

    raw_scores = (
        jnp.einsum("thd,uhd->htu", heads_query, heads_key, preferred_element_type=jnp.float32)
        * score_scale
    )
    scores = jnp.where(mask[None], raw_scores, NEG_FILL)
    row_peak = jnp.max(scores, axis=2)
    expo = jnp.where(mask[None], jnp.exp(scores - row_peak[..., None]), 0.0)
    row_total = jnp.sum(expo, axis=2)
    prob = expo / row_total[..., None]
    weights = prob.astype(jnp.bfloat16)
    attended = jnp.einsum("htu,uhd->thd", weights, heads_value, preferred_element_type=jnp.float32)

    flattened = attended.reshape(row_count, channels)
    position = jnp.arange(row_count, dtype=jnp.int32) % BLK
    chosen = jnp.any(jnp.repeat(mask_pos, BLK, axis=0) == position[:, None], axis=1)
    weighted = flattened * gain
    sums = pair_sum(
        jnp.stack(
            [
                jnp.sum(flattened * flattened, axis=1),
                jnp.sum(weighted * weighted, axis=1),
                jnp.sum(teacher.astype(jnp.float32) * weighted, axis=1),
            ]
        ),
        "head",
    )
    squares = sums[0]
    inverse = lax.rsqrt(squares / D + NORM_EPS)
    prediction = flattened * inverse[:, None] * gain
    residual = jnp.where(chosen[:, None], prediction - teacher.astype(jnp.float32), 0.0)
    scaled = residual * gain
    cross_term = jnp.where(chosen, inverse * sums[1] - sums[2], 0.0)
    out_grad = (
        inverse[:, None] * scaled - flattened * (inverse**3 * cross_term / D)[:, None]
    ).astype(jnp.bfloat16)
    heads_grad = split_heads(out_grad)
    delta = jnp.sum(heads_grad.astype(jnp.float32) * attended, axis=2).T

    prob_grad = jnp.einsum("thd,uhd->htu", heads_grad, heads_value, preferred_element_type=jnp.float32)
    score_grad = (prob * (prob_grad - delta[:, :, None])).astype(jnp.bfloat16)
    query_grad = (
        jnp.einsum("htu,uhd->thd", score_grad, heads_key, preferred_element_type=jnp.float32)
        * score_scale
    )
    key_part = (
        jnp.einsum("htu,thd->uhd", score_grad, heads_query, preferred_element_type=jnp.float32)
        * score_scale
    ).reshape(key_count, channels)
    value_part = jnp.einsum(
        "htu,thd->uhd", weights, heads_grad, preferred_element_type=jnp.float32
    ).reshape(key_count, channels)

    local_taps = jnp.stack(
        [
            jnp.sum(
                value_part
                * vin_win[far_lead - tap_index : far_lead - tap_index + key_count].astype(jnp.float32),
                axis=0,
            )
            for tap_index in range(tap_count)
        ]
    )
    conv_grad = all_sum(local_taps, "tm")

    lead = jnp.zeros((far_lead, channels), jnp.float32)
    padded_value = jnp.concatenate([lead, value_part, jnp.zeros((rim_rows, channels), jnp.float32)], 0)
    value_sum = jnp.zeros((key_count + far_lead, channels), jnp.float32)
    for tap_index in range(tap_count):
        value_sum = value_sum + conv_weight[tap_index] * padded_value[tap_index : tap_index + key_count + far_lead]

    def relay_back(grads):
        cut_third = row_count - far_rows + far_lead
        grad_third = grads[:cut_third]
        grad_second = grads[cut_third : cut_third + row_count]
        grad_first = grads[cut_third + row_count : cut_third + 2 * row_count]
        grad_own = grads[cut_third + 2 * row_count :]
        back_third = from_behind(grad_third.astype(jnp.bfloat16), "tm", -1).astype(jnp.float32)
        back_first = chip_swap(grad_first.astype(jnp.bfloat16), "tm").astype(jnp.float32)
        grad_second = grad_second + jnp.concatenate(
            [jnp.zeros((far_rows - far_lead, grads.shape[1]), jnp.float32), back_third], 0
        )
        grad_second = grad_second + jnp.where(even, 0.0, back_first)
        back_second = from_behind(grad_second.astype(jnp.bfloat16), "tm", -2).astype(jnp.float32)
        return grad_own + jnp.where(even, back_first, 0.0) + back_second

    value_total = relay_back(value_sum)
    key_total = relay_back(jnp.concatenate([lead, key_part], 0))

    return (
        query_grad.reshape(row_count, channels).astype(jnp.bfloat16),
        key_total.astype(jnp.bfloat16),
        value_total.astype(jnp.bfloat16),
        conv_grad,
    )


def solution(mesh):
    placed = (
        P("tm", "head"),
        P("tm", "head"),
        P("tm", "head"),
        P("tm", "head"),
        P("head"),
        P(None, "head"),
        P("tm", None),
        P("tm", None),
    )
    return jax.shard_map(
        body,
        mesh=mesh,
        in_specs=placed,
        out_specs=(P("tm", "head"), P("tm", "head"), P("tm", "head"), P(None, "head")),
        check_vma=False,
    )
```

```python
import jax
import jax.numpy as jnp
from jax import lax
from jax.sharding import PartitionSpec as P

D = 2048
HD = 128
BLK = 128
REACH = 3
WIN = 6


NEG_FILL = -1e30
NORM_EPS = 1e-06


def from_behind(block, axis, distance):
    devices = range(lax.axis_size(axis))
    route = [(i - distance, i) for i in devices if i - distance in devices]
    return lax.ppermute(block, axis, route)


def chip_swap(block, axis):
    size = lax.axis_size(axis)
    return lax.ppermute(block, axis, [(i, i ^ 1) for i in range(size)])


def all_sum(block, axis):
    size = lax.axis_size(axis)
    if size & (size - 1):
        return lax.psum(block, axis)
    stride = 1
    while stride < size:
        block = block + lax.ppermute(block, axis, [(i, i ^ stride) for i in range(size)])
        stride *= 2
    return block


def pair_sum(block, axis):
    if lax.axis_size(axis) != 2:
        return lax.psum(block, axis)
    return block + lax.ppermute(block, axis, [(0, 1), (1, 0)])


def split_heads(array):
    return array.reshape(array.shape[0], array.shape[1] // HD, HD)


def window_mask(block_bits, device, row_count, key_count):
    per_device = row_count // BLK
    key_blocks = key_count // BLK
    first_block = device * per_device - (key_blocks - per_device)
    qb = jnp.arange(per_device, dtype=jnp.int32)
    kb = jnp.arange(key_blocks, dtype=jnp.int32)
    relative = qb[:, None] + (key_blocks - per_device) - kb[None, :]
    one_hot = relative[:, :, None] == jnp.arange(WIN, dtype=jnp.int32)[None, None, :]
    picked_bits = jnp.sum(jnp.where(one_hot, block_bits[:, None, :], 0), axis=2)
    coarse = (picked_bits > 0) & (relative >= 0) & (relative < WIN) & (first_block + kb[None, :] >= 0)
    fine = jnp.repeat(jnp.repeat(coarse, BLK, axis=0), BLK, axis=1)
    q = jnp.arange(row_count, dtype=jnp.int32)
    s = jnp.arange(key_count, dtype=jnp.int32)
    causal = s[None, :] <= q[:, None] + (key_count - row_count)
    return fine & causal


def body(queries, keys, values_in, teacher, gain, conv_weight, block_bits, mask_pos):
    row_count, channels = queries.shape
    tap_count = conv_weight.shape[0]
    rim_rows = tap_count - 1
    device = lax.axis_index("tm")
    even = device % 2 == 0
    score_scale = HD ** (-0.5)
    far_rows = row_count - BLK
    far_lead = 8
    key_count = REACH * row_count + (row_count - far_rows)

    def relay(own, direct_third=False):
        second = from_behind(own, "tm", 2)
        first = chip_swap(jnp.where(even, own, second), "tm")
        if direct_third:
            third = from_behind(own[far_rows - far_lead :], "tm", REACH)
        else:
            third = from_behind(second[far_rows - far_lead :], "tm", 1)
        return jnp.concatenate([third, second, first, own], 0)

    key_win = relay(keys, direct_third=True)[far_lead:]
    vin_win = relay(values_in)

    conv_sum = jnp.zeros((key_count, channels), jnp.float32)
    for tap_index in range(tap_count):
        conv_sum = conv_sum + conv_weight[tap_index] * vin_win[
            far_lead - tap_index : far_lead - tap_index + key_count
        ].astype(jnp.float32)
    value_win = conv_sum.astype(jnp.bfloat16)

    heads_query = split_heads(queries)
    heads_key = split_heads(key_win)
    heads_value = split_heads(value_win)
    mask = window_mask(block_bits, device, row_count, key_count)

    raw_scores = (
        jnp.einsum("thd,uhd->htu", heads_query, heads_key, preferred_element_type=jnp.float32)
        * score_scale
    )
    scores = jnp.where(mask[None], raw_scores, NEG_FILL)
    row_peak = jnp.max(scores, axis=2)
    expo = jnp.where(mask[None], jnp.exp(scores - row_peak[..., None]), 0.0)
    row_total = jnp.sum(expo, axis=2)
    prob = expo / row_total[..., None]
    weights = prob.astype(jnp.bfloat16)
    attended = jnp.einsum("htu,uhd->thd", weights, heads_value, preferred_element_type=jnp.float32)

    flattened = attended.reshape(row_count, channels)
    position = jnp.arange(row_count, dtype=jnp.int32) % BLK
    chosen = jnp.any(jnp.repeat(mask_pos, BLK, axis=0) == position[:, None], axis=1)
    weighted = flattened * gain
    sums = pair_sum(
        jnp.stack(
            [
                jnp.sum(flattened * flattened, axis=1),
                jnp.sum(weighted * weighted, axis=1),
                jnp.sum(teacher.astype(jnp.float32) * weighted, axis=1),
            ]
        ),
        "head",
    )
    squares = sums[0]
    inverse = lax.rsqrt(squares / D + NORM_EPS)
    prediction = flattened * inverse[:, None] * gain
    residual = jnp.where(chosen[:, None], prediction - teacher.astype(jnp.float32), 0.0)
    scaled = residual * gain
    cross_term = jnp.where(chosen, inverse * sums[1] - sums[2], 0.0)
    out_grad = (
        inverse[:, None] * scaled - flattened * (inverse**3 * cross_term / D)[:, None]
    ).astype(jnp.bfloat16)
    heads_grad = split_heads(out_grad)
    delta = jnp.sum(heads_grad.astype(jnp.float32) * attended, axis=2).T

    prob_grad = jnp.einsum("thd,uhd->htu", heads_grad, heads_value, preferred_element_type=jnp.float32)
    score_grad = (prob * (prob_grad - delta[:, :, None])).astype(jnp.bfloat16)
    query_grad = (
        jnp.einsum("htu,uhd->thd", score_grad, heads_key, preferred_element_type=jnp.float32)
        * score_scale
    )
    key_part = (
        jnp.einsum("htu,thd->uhd", score_grad, heads_query, preferred_element_type=jnp.float32)
        * score_scale
    ).reshape(key_count, channels)
    value_part = jnp.einsum(
        "htu,thd->uhd", weights, heads_grad, preferred_element_type=jnp.float32
    ).reshape(key_count, channels)

    local_taps = jnp.stack(
        [
            jnp.sum(
                value_part
                * vin_win[far_lead - tap_index : far_lead - tap_index + key_count].astype(jnp.float32),
                axis=0,
            )
            for tap_index in range(tap_count)
        ]
    )
    conv_grad = all_sum(local_taps, "tm")

    lead = jnp.zeros((far_lead, channels), jnp.float32)
    padded_value = jnp.concatenate([lead, value_part, jnp.zeros((rim_rows, channels), jnp.float32)], 0)
    value_sum = jnp.zeros((key_count + far_lead, channels), jnp.float32)
    for tap_index in range(tap_count):
        value_sum = value_sum + conv_weight[tap_index] * padded_value[tap_index : tap_index + key_count + far_lead]

    def relay_back(grads):
        cut_third = row_count - far_rows + far_lead
        grad_third = grads[:cut_third]
        grad_second = grads[cut_third : cut_third + row_count]
        grad_first = grads[cut_third + row_count : cut_third + 2 * row_count]
        grad_own = grads[cut_third + 2 * row_count :]
        back_third = from_behind(grad_third.astype(jnp.bfloat16), "tm", -1).astype(jnp.float32)
        back_first = chip_swap(grad_first.astype(jnp.bfloat16), "tm").astype(jnp.float32)
        grad_second = grad_second + jnp.concatenate(
            [jnp.zeros((far_rows - far_lead, grads.shape[1]), jnp.float32), back_third], 0
        )
        grad_second = grad_second + jnp.where(even, 0.0, back_first)
        back_second = from_behind(grad_second.astype(jnp.bfloat16), "tm", -2).astype(jnp.float32)
        return grad_own + jnp.where(even, back_first, 0.0) + back_second

    value_total = relay_back(value_sum)
    key_total = relay_back(jnp.concatenate([lead, key_part], 0))

    return (
        query_grad.reshape(row_count, channels).astype(jnp.bfloat16),
        key_total.astype(jnp.bfloat16),
        value_total.astype(jnp.bfloat16),
        conv_grad,
    )


def solution(mesh):
    placed = (
        P("tm", "head"),
        P("tm", "head"),
        P("tm", "head"),
        P("tm", "head"),
        P("head"),
        P(None, "head"),
        P("tm", None),
        P("tm", None),
    )
    return jax.shard_map(
        body,
        mesh=mesh,
        in_specs=placed,
        out_specs=(P("tm", "head"), P("tm", "head"), P("tm", "head"), P(None, "head")),
        check_vma=False,
    )
```

```python
import jax
import jax.numpy as jnp
from jax import lax
from jax.sharding import PartitionSpec as P

D = 2048
HD = 128
BLK = 128
REACH = 3
WIN = 6


NEG_FILL = -1e30
NORM_EPS = 1e-06


def from_behind(block, axis, distance):
    devices = range(lax.axis_size(axis))
    route = [(i - distance, i) for i in devices if i - distance in devices]
    return lax.ppermute(block, axis, route)


def chip_swap(block, axis):
    size = lax.axis_size(axis)
    return lax.ppermute(block, axis, [(i, i ^ 1) for i in range(size)])


def all_sum(block, axis):
    size = lax.axis_size(axis)
    if size & (size - 1):
        return lax.psum(block, axis)
    stride = 1
    while stride < size:
        block = block + lax.ppermute(block, axis, [(i, i ^ stride) for i in range(size)])
        stride *= 2
    return block


def pair_sum(block, axis):
    if lax.axis_size(axis) != 2:
        return lax.psum(block, axis)
    return block + lax.ppermute(block, axis, [(0, 1), (1, 0)])


def split_heads(array):
    return array.reshape(array.shape[0], array.shape[1] // HD, HD)


def window_mask(block_bits, device, row_count, key_count):
    per_device = row_count // BLK
    key_blocks = key_count // BLK
    first_block = device * per_device - (key_blocks - per_device)
    qb = jnp.arange(per_device, dtype=jnp.int32)
    kb = jnp.arange(key_blocks, dtype=jnp.int32)
    relative = qb[:, None] + (key_blocks - per_device) - kb[None, :]
    one_hot = relative[:, :, None] == jnp.arange(WIN, dtype=jnp.int32)[None, None, :]
    picked_bits = jnp.sum(jnp.where(one_hot, block_bits[:, None, :], 0), axis=2)
    coarse = (picked_bits > 0) & (relative >= 0) & (relative < WIN) & (first_block + kb[None, :] >= 0)
    fine = jnp.repeat(jnp.repeat(coarse, BLK, axis=0), BLK, axis=1)
    q = jnp.arange(row_count, dtype=jnp.int32)
    s = jnp.arange(key_count, dtype=jnp.int32)
    causal = s[None, :] <= q[:, None] + (key_count - row_count)
    return fine & causal


def body(queries, keys, values_in, teacher, gain, conv_weight, block_bits, mask_pos):
    row_count, channels = queries.shape
    tap_count = conv_weight.shape[0]
    rim_rows = tap_count - 1
    device = lax.axis_index("tm")
    even = device % 2 == 0
    score_scale = HD ** (-0.5)
    far_rows = row_count - BLK
    far_lead = 8
    key_count = REACH * row_count + (row_count - far_rows)

    def relay(own, lead_rows):
        second = from_behind(own, "tm", 2)
        first = chip_swap(jnp.where(even, own, second), "tm")
        third = from_behind(second[far_rows - lead_rows :], "tm", 1)
        return jnp.concatenate([third, second, first, own], 0)

    key_win = relay(keys, 0)
    vin_win = relay(values_in, far_lead)

    conv_sum = jnp.zeros((key_count, channels), jnp.float32)
    for tap_index in range(tap_count):
        conv_sum = conv_sum + conv_weight[tap_index] * vin_win[
            far_lead - tap_index : far_lead - tap_index + key_count
        ].astype(jnp.float32)
    value_win = conv_sum.astype(jnp.bfloat16)

    heads_query = split_heads(queries)
    heads_key = split_heads(key_win)
    heads_value = split_heads(value_win)
    mask = window_mask(block_bits, device, row_count, key_count)

    raw_scores = (
        jnp.einsum("thd,uhd->htu", heads_query, heads_key, preferred_element_type=jnp.float32)
        * score_scale
    )
    scores = jnp.where(mask[None], raw_scores, NEG_FILL)
    row_peak = jnp.max(scores, axis=2)
    expo = jnp.where(mask[None], jnp.exp(scores - row_peak[..., None]), 0.0)
    row_total = jnp.sum(expo, axis=2)
    prob = expo / row_total[..., None]
    weights = prob.astype(jnp.bfloat16)
    attended = jnp.einsum("htu,uhd->thd", weights, heads_value, preferred_element_type=jnp.float32)

    flattened = attended.reshape(row_count, channels)
    position = jnp.arange(row_count, dtype=jnp.int32) % BLK
    chosen = jnp.any(jnp.repeat(mask_pos, BLK, axis=0) == position[:, None], axis=1)
    weighted = flattened * gain
    sums = pair_sum(
        jnp.stack(
            [
                jnp.sum(flattened * flattened, axis=1),
                jnp.sum(weighted * weighted, axis=1),
                jnp.sum(teacher.astype(jnp.float32) * weighted, axis=1),
            ]
        ),
        "head",
    )
    squares = sums[0]
    inverse = lax.rsqrt(squares / D + NORM_EPS)
    prediction = flattened * inverse[:, None] * gain
    residual = jnp.where(chosen[:, None], prediction - teacher.astype(jnp.float32), 0.0)
    scaled = residual * gain
    cross_term = jnp.where(chosen, inverse * sums[1] - sums[2], 0.0)
    out_grad = (
        inverse[:, None] * scaled - flattened * (inverse**3 * cross_term / D)[:, None]
    ).astype(jnp.bfloat16)
    heads_grad = split_heads(out_grad)
    delta = jnp.sum(heads_grad.astype(jnp.float32) * attended, axis=2).T

    prob_grad = jnp.einsum("thd,uhd->htu", heads_grad, heads_value, preferred_element_type=jnp.float32)
    score_grad = (prob * (prob_grad - delta[:, :, None])).astype(jnp.bfloat16)
    query_grad = (
        jnp.einsum("htu,uhd->thd", score_grad, heads_key, preferred_element_type=jnp.float32)
        * score_scale
    )
    key_part = (
        jnp.einsum("htu,thd->uhd", score_grad, heads_query, preferred_element_type=jnp.float32)
        * score_scale
    ).reshape(key_count, channels)
    value_part = jnp.einsum(
        "htu,thd->uhd", weights, heads_grad, preferred_element_type=jnp.float32
    ).reshape(key_count, channels)

    local_taps = jnp.stack(
        [
            jnp.sum(
                value_part
                * vin_win[far_lead - tap_index : far_lead - tap_index + key_count].astype(jnp.float32),
                axis=0,
            )
            for tap_index in range(tap_count)
        ]
    )
    conv_grad = all_sum(local_taps, "tm")

    lead = jnp.zeros((far_lead, channels), jnp.float32)
    padded_value = jnp.concatenate([lead, value_part, jnp.zeros((rim_rows, channels), jnp.float32)], 0)
    value_sum = jnp.zeros((key_count + far_lead, channels), jnp.float32)
    for tap_index in range(tap_count):
        value_sum = value_sum + conv_weight[tap_index] * padded_value[tap_index : tap_index + key_count + far_lead]

    def relay_back(grads):
        cut_third = row_count - far_rows + far_lead
        grad_third = grads[:cut_third]
        grad_second = grads[cut_third : cut_third + row_count]
        grad_first = grads[cut_third + row_count : cut_third + 2 * row_count]
        grad_own = grads[cut_third + 2 * row_count :]
        back_third = from_behind(grad_third.astype(jnp.bfloat16), "tm", -1).astype(jnp.float32)
        back_first = chip_swap(grad_first.astype(jnp.bfloat16), "tm").astype(jnp.float32)
        grad_second = grad_second + jnp.concatenate(
            [jnp.zeros((far_rows - far_lead, grads.shape[1]), jnp.float32), back_third], 0
        )
        grad_second = grad_second + jnp.where(even, 0.0, back_first)
        back_second = from_behind(grad_second.astype(jnp.bfloat16), "tm", -2).astype(jnp.float32)
        return grad_own + jnp.where(even, back_first, 0.0) + back_second

    value_total = relay_back(value_sum)
    key_total = relay_back(jnp.concatenate([lead, key_part], 0))

    return (
        query_grad.reshape(row_count, channels).astype(jnp.bfloat16),
        key_total.astype(jnp.bfloat16),
        value_total.astype(jnp.bfloat16),
        conv_grad,
    )


def solution(mesh):
    placed = (
        P("tm", "head"),
        P("tm", "head"),
        P("tm", "head"),
        P("tm", "head"),
        P("head"),
        P(None, "head"),
        P("tm", None),
        P("tm", None),
    )
    return jax.shard_map(
        body,
        mesh=mesh,
        in_specs=placed,
        out_specs=(P("tm", "head"), P("tm", "head"), P("tm", "head"), P(None, "head")),
        check_vma=False,
    )
```

```python
import jax
import jax.numpy as jnp
from jax import lax
from jax.sharding import PartitionSpec as P

D = 2048
HD = 128
BLK = 128
REACH = 3
WIN = 6


NEG_FILL = -1e30
NORM_EPS = 1e-06


def from_behind(block, axis, distance):
    devices = range(lax.axis_size(axis))
    route = [(i - distance, i) for i in devices if i - distance in devices]
    return lax.ppermute(block, axis, route)


def chip_swap(block, axis):
    size = lax.axis_size(axis)
    return lax.ppermute(block, axis, [(i, i ^ 1) for i in range(size)])


def all_sum(block, axis):
    size = lax.axis_size(axis)
    if size & (size - 1):
        return lax.psum(block, axis)
    stride = 1
    while stride < size:
        block = block + lax.ppermute(block, axis, [(i, i ^ stride) for i in range(size)])
        stride *= 2
    return block


def pair_sum(block, axis):
    if lax.axis_size(axis) != 2:
        return lax.psum(block, axis)
    return block + lax.ppermute(block, axis, [(0, 1), (1, 0)])


def split_heads(array):
    return array.reshape(array.shape[0], array.shape[1] // HD, HD)


def window_mask(block_bits, device, row_count, key_count):
    per_device = row_count // BLK
    key_blocks = key_count // BLK
    first_block = device * per_device - (key_blocks - per_device)
    qb = jnp.arange(per_device, dtype=jnp.int32)
    kb = jnp.arange(key_blocks, dtype=jnp.int32)
    relative = qb[:, None] + (key_blocks - per_device) - kb[None, :]
    one_hot = relative[:, :, None] == jnp.arange(WIN, dtype=jnp.int32)[None, None, :]
    picked_bits = jnp.sum(jnp.where(one_hot, block_bits[:, None, :], 0), axis=2)
    coarse = (picked_bits > 0) & (relative >= 0) & (relative < WIN) & (first_block + kb[None, :] >= 0)
    fine = jnp.repeat(jnp.repeat(coarse, BLK, axis=0), BLK, axis=1)
    q = jnp.arange(row_count, dtype=jnp.int32)
    s = jnp.arange(key_count, dtype=jnp.int32)
    causal = s[None, :] <= q[:, None] + (key_count - row_count)
    return fine & causal


def body(queries, keys, values_in, teacher, gain, conv_weight, block_bits, mask_pos):
    row_count, channels = queries.shape
    tap_count = conv_weight.shape[0]
    rim_rows = tap_count - 1
    device = lax.axis_index("tm")
    even = device % 2 == 0
    score_scale = HD ** (-0.5)
    far_rows = row_count - BLK
    far_lead = 8
    key_count = REACH * row_count + (row_count - far_rows)

    def relay(own, lead_rows):
        second = from_behind(own, "tm", 2)
        first = chip_swap(jnp.where(even, own, second), "tm")
        third = from_behind(second[far_rows - lead_rows :], "tm", 1)
        return jnp.concatenate([third, second, first, own], 0)

    key_win = relay(keys, 0)
    vin_win = relay(values_in, far_lead)

    conv_sum = jnp.zeros((key_count, channels), jnp.float32)
    for tap_index in range(tap_count):
        conv_sum = conv_sum + conv_weight[tap_index] * vin_win[
            far_lead - tap_index : far_lead - tap_index + key_count
        ].astype(jnp.float32)
    value_win = conv_sum.astype(jnp.bfloat16)

    heads_query = split_heads(queries)
    heads_key = split_heads(key_win)
    heads_value = split_heads(value_win)
    mask = window_mask(block_bits, device, row_count, key_count)

    raw_scores = (
        jnp.einsum("thd,uhd->htu", heads_query, heads_key, preferred_element_type=jnp.float32)
        * score_scale
    )
    scores = jnp.where(mask[None], raw_scores, NEG_FILL)
    row_peak = jnp.max(scores, axis=2)
    expo = jnp.where(mask[None], jnp.exp(scores - row_peak[..., None]), 0.0)
    row_total = jnp.sum(expo, axis=2)
    prob = expo / row_total[..., None]
    weights = prob.astype(jnp.bfloat16)
    attended = jnp.einsum("htu,uhd->thd", weights, heads_value, preferred_element_type=jnp.float32)

    flattened = attended.reshape(row_count, channels)
    position = jnp.arange(row_count, dtype=jnp.int32) % BLK
    chosen = jnp.any(jnp.repeat(mask_pos, BLK, axis=0) == position[:, None], axis=1)
    weighted = flattened * gain
    sums = pair_sum(
        jnp.stack(
            [
                jnp.sum(flattened * flattened, axis=1),
                jnp.sum(weighted * weighted, axis=1),
                jnp.sum(teacher.astype(jnp.float32) * weighted, axis=1),
            ]
        ),
        "head",
    )
    squares = sums[0]
    inverse = lax.rsqrt(squares / D + NORM_EPS)
    prediction = flattened * inverse[:, None] * gain
    residual = jnp.where(chosen[:, None], prediction - teacher.astype(jnp.float32), 0.0)
    scaled = residual * gain
    cross_term = jnp.where(chosen, inverse * sums[1] - sums[2], 0.0)
    out_grad = (
        inverse[:, None] * scaled - flattened * (inverse**3 * cross_term / D)[:, None]
    ).astype(jnp.bfloat16)
    heads_grad = split_heads(out_grad)
    delta = jnp.sum(heads_grad.astype(jnp.float32) * attended, axis=2).T

    prob_grad = jnp.einsum("thd,uhd->htu", heads_grad, heads_value, preferred_element_type=jnp.float32)
    score_grad = (prob * (prob_grad - delta[:, :, None])).astype(jnp.bfloat16)
    query_grad = (
        jnp.einsum("htu,uhd->thd", score_grad, heads_key, preferred_element_type=jnp.float32)
        * score_scale
    )
    key_part = (
        jnp.einsum("htu,thd->uhd", score_grad, heads_query, preferred_element_type=jnp.float32)
        * score_scale
    ).reshape(key_count, channels)
    value_part = jnp.einsum(
        "htu,thd->uhd", weights, heads_grad, preferred_element_type=jnp.float32
    ).reshape(key_count, channels)

    local_taps = jnp.stack(
        [
            jnp.sum(
                value_part
                * vin_win[far_lead - tap_index : far_lead - tap_index + key_count].astype(jnp.float32),
                axis=0,
            )
            for tap_index in range(tap_count)
        ]
    )
    conv_grad = all_sum(local_taps, "tm")

    lead = jnp.zeros((far_lead, channels), jnp.float32)
    padded_value = jnp.concatenate([lead, value_part, jnp.zeros((rim_rows, channels), jnp.float32)], 0)
    value_sum = jnp.zeros((key_count + far_lead, channels), jnp.float32)
    for tap_index in range(tap_count):
        value_sum = value_sum + conv_weight[tap_index] * padded_value[tap_index : tap_index + key_count + far_lead]

    def relay_back(grads, lead_rows):
        cut_third = row_count - far_rows + lead_rows
        grad_third = grads[:cut_third]
        grad_second = grads[cut_third : cut_third + row_count]
        grad_first = grads[cut_third + row_count : cut_third + 2 * row_count]
        grad_own = grads[cut_third + 2 * row_count :]
        back_third = from_behind(grad_third.astype(jnp.bfloat16), "tm", -1).astype(jnp.float32)
        back_first = chip_swap(grad_first.astype(jnp.bfloat16), "tm").astype(jnp.float32)
        grad_second = grad_second + jnp.concatenate(
            [jnp.zeros((far_rows - lead_rows, grads.shape[1]), jnp.float32), back_third], 0
        )
        grad_second = grad_second + jnp.where(even, 0.0, back_first)
        back_second = from_behind(grad_second.astype(jnp.bfloat16), "tm", -2).astype(jnp.float32)
        return grad_own + jnp.where(even, back_first, 0.0) + back_second

    value_total = relay_back(value_sum, far_lead)
    key_total = relay_back(key_part, 0)

    return (
        query_grad.reshape(row_count, channels).astype(jnp.bfloat16),
        key_total.astype(jnp.bfloat16),
        value_total.astype(jnp.bfloat16),
        conv_grad,
    )


def solution(mesh):
    placed = (
        P("tm", "head"),
        P("tm", "head"),
        P("tm", "head"),
        P("tm", "head"),
        P("head"),
        P(None, "head"),
        P("tm", None),
        P("tm", None),
    )
    return jax.shard_map(
        body,
        mesh=mesh,
        in_specs=placed,
        out_specs=(P("tm", "head"), P("tm", "head"), P("tm", "head"), P(None, "head")),
        check_vma=False,
    )
```
